128 devices in a mesh: lm: 16 (over y, x), kf: 8 (over z, core).
Axes of the slice: x: 4, y: 4, z: 4, core: 2. Of those that a mesh axis runs over, the one named last changes fastest.
Arguments:
- land_rhs: float32 [3, 524288], P(None, ('lm', 'kf')), may hold values from -6 to 6
- key_rhs: float32 [15, 65536], P(None, ('lm', 'kf')), may hold values from -6 to 6
- land_damp: float32 [3, 524288], P(None, ('lm', 'kf')), may hold values from 0.5 to 2
- key_damp: float32 [15, 65536], P(None, ('lm', 'kf')), may hold values from 0.5 to 2
- land_jac: float32 [6, 2097152], P(None, ('lm', 'kf')), may hold values from -4 to 4
- key_jac: float32 [30, 2097152], P(None, ('lm', 'kf')), may hold values from -1.5 to 1.5
- obs_landmark: int32 [2097152], P(('lm', 'kf')), may hold values from 0 to 32767, as said below
- obs_keyframe: int32 [2097152], P(('lm', 'kf')), may hold values from 0 to 65535, as said below
- live_blocks: int32 [128], P(('lm', 'kf')), may hold values from 32 to 128, as said below
- preint: float32 [240, 983040], P(None, ('lm', 'kf')), as said below
Outputs:
- sol_land: float32 [3, 524288], P(None, ('lm', 'kf'))
- sol_key: float32 [15, 65536], P(None, ('lm', 'kf'))
The draws below stay inside these ranges and needn't reach their ends.
Inputs may be any that keep to these rules, and one draw needn't show every extreme that they name: `obs_landmark`: offsets among the 32768 landmarks of the lm index of the device holding the row. `obs_keyframe`: row o names a state s whose device index (s // 512) has the same kf index as the device holding row o. `live_blocks`: blocks past a device's count are padding; some device uses all its blocks. `preint`: each window's block is symmetric, and its diagonal exceeds the sum of magnitudes off the diagonal in its row.
All inputs are finite; a program needn't handle non-finite values.
Results may differ from the reference program's by a relative error of at most 0.0001.
Values sent between devices are 32-bit elements; how exact they have to be, the bound alone decides.
No kernel may reach another device: no remote copies, remote signals or barrier semaphores. Data moves between devices by JAX's collectives and lax.ppermute only.
A program may use at most 128 MiB of HBM per device.

```python
import math
import jax
import jax.numpy as jnp
from jax import lax

WSTATES = 16
SDIM = 15
BLOCK = 128
OBLK = 128
ITERS = 2
LM_GROUPS = 16
KF_GROUPS = 8
LDEV = 4096
SDEV = 512
WPAR = 240
LANDMARKS = 524288
STATES = 65536
WINDOWS = 4096
OBS = 2097152


def draw_obs_landmark(key, part):
    count = OBLK * BLOCK * LM_GROUPS * KF_GROUPS
    return jax.random.randint(jax.random.fold_in(key, 11), (count,), 0, KF_GROUPS * LDEV, dtype=jnp.int32)


def draw_obs_keyframe(key, part):
    count = OBLK * BLOCK * LM_GROUPS * KF_GROUPS
    row_ids = jnp.arange(count, dtype=jnp.int32)
    kf_col = row_ids // (OBLK * BLOCK) % KF_GROUPS
    first_key = jax.random.fold_in(key, 21)
    second_key = jax.random.fold_in(key, 22)
    lm_pick = jax.random.randint(first_key, (count,), 0, LM_GROUPS, dtype=jnp.int32)
    offset = jax.random.randint(second_key, (count,), 0, SDEV, dtype=jnp.int32)
    return (lm_pick * KF_GROUPS + kf_col) * SDEV + offset


def draw_live_blocks(key, part):
    first_key = jax.random.fold_in(key, 31)
    second_key = jax.random.fold_in(key, 32)
    devices = LM_GROUPS * KF_GROUPS
    lowest = max(1, OBLK // 4)
    counts = jax.random.randint(first_key, (devices,), lowest, OBLK + 1, dtype=jnp.int32)
    position = jax.random.randint(second_key, (), 0, devices, dtype=jnp.int32)
    return counts.at[position].set(OBLK)


def draw_preint(key, part):
    first_key = jax.random.fold_in(key, 41)
    second_key = jax.random.fold_in(key, 42)
    random_part = jax.random.uniform(first_key, (WINDOWS, WPAR, WPAR), jnp.float32, -1.0, 1.0) / (WPAR - 1)
    symmetric = 0.5 * (random_part + jnp.swapaxes(random_part, 1, 2))
    identity = jnp.eye(WPAR, dtype=jnp.float32)
    diagonal = jax.random.uniform(second_key, (WINDOWS, WPAR), jnp.float32, 1.1, 2.2)
    blocks = symmetric * (1.0 - identity) + identity * diagonal[:, :, None]
    return blocks.transpose(1, 0, 2).reshape(WPAR, WINDOWS * WPAR)


def levels(rng, shape, pieces, least, high):
    loudness, own = 1.0, jax.random.fold_in(rng, 6)
    for dim, parts in pieces:
        draws = jnp.exp(jax.random.uniform(jax.random.fold_in(own, dim), (parts,), jnp.float32, least / len(pieces), high / len(pieces)))
        loudness = loudness * jnp.repeat(draws, shape[dim] // parts).reshape([-1 if axis == dim else 1 for axis in range(len(shape))])
    return loudness


def bell_draw(own_key, extent, scale, limit, cuts=(), kind=jnp.bfloat16):
    array = scale * jax.random.normal(own_key, extent, jnp.float32)
    if cuts:
        array = array * levels(own_key, extent, cuts, -0.22, 0.18)
    return jnp.clip(array, -limit, limit).astype(kind)


def setup_inputs(seed: int = 0) -> dict:
    keys = jax.random.split(jax.random.key(seed), 11)
    return {
        "land_rhs": bell_draw(keys[0], (3, LANDMARKS), 1.0, 6.0, ((1, 128),), jnp.float32),
        "key_rhs": bell_draw(keys[1], (SDIM, STATES), 1.0, 6.0, ((1, 128),), jnp.float32),
        "land_damp": jnp.clip(jnp.exp(math.log(2.0) - 1.3862944 * jax.random.uniform(keys[2], (3, LANDMARKS), jnp.float32) ** levels(keys[2], (3, LANDMARKS), ((1, 128),), -0.2, 0.2)), 0.5, 2.0),
        "key_damp": jnp.clip(jnp.exp(math.log(2.0) - 1.3862944 * jax.random.uniform(keys[3], (SDIM, STATES), jnp.float32) ** levels(keys[3], (SDIM, STATES), ((1, 128),), -0.2, 0.2)), 0.5, 2.0),
        "land_jac": bell_draw(keys[4], (6, OBS), 0.3, 4.0, ((1, 128),), jnp.float32),
        "key_jac": bell_draw(keys[5], (2 * SDIM, OBS), 0.1, 1.5, ((1, 128),), jnp.float32),
        "obs_landmark": draw_obs_landmark(jax.random.fold_in(keys[10], 71), 0),
        "obs_keyframe": draw_obs_keyframe(jax.random.fold_in(keys[10], 71), 0),
        "live_blocks": draw_live_blocks(jax.random.fold_in(keys[10], 71), 0),
        "preint": draw_preint(jax.random.fold_in(keys[10], 71), 0),
    }


def window_product(preint, vectors):
    windows = preint.shape[1] // WPAR
    blocks = preint.reshape(WPAR, windows, WPAR)
    stacked = vectors.reshape(SDIM, windows, WSTATES).transpose(1, 2, 0).reshape(windows, WPAR)
    mapped = jnp.einsum("awb,wb->wa", blocks, stacked, precision=lax.Precision.HIGHEST)
    return mapped.reshape(windows, WSTATES, SDIM).transpose(2, 0, 1).reshape(SDIM, windows * WSTATES)


def normal_product(dir_land, dir_key, land_jac, key_jac, obs_landmark, obs_keyframe, validity, preint, land_damp, key_damp):
    count = land_jac.shape[1]
    land_rows = land_jac.reshape(2, 3, count)
    key_rows = key_jac.reshape(2, SDIM, count)
    seen_land = dir_land[:, obs_landmark]
    seen_key = dir_key[:, obs_keyframe]
    image = jnp.sum(land_rows * seen_land[None], axis=1) + jnp.sum(key_rows * seen_key[None], axis=1)
    image = image * validity[None]
    back_land = jnp.sum(land_rows * image[:, None], axis=0)
    back_key = jnp.sum(key_rows * image[:, None], axis=0)
    prod_land = jnp.zeros_like(dir_land).at[:, obs_landmark].add(back_land) + land_damp * dir_land
    prod_key = jnp.zeros_like(dir_key).at[:, obs_keyframe].add(back_key) + key_damp * dir_key + window_product(preint, dir_key)
    return prod_land, prod_key


def reference(land_rhs, key_rhs, land_damp, key_damp, land_jac, key_jac, obs_landmark, obs_keyframe, live_blocks, preint):
    per_device = OBLK * BLOCK
    row_ids = jnp.arange(land_jac.shape[1], dtype=jnp.int32)
    owner = row_ids // per_device
    block_ids = (row_ids % per_device) // BLOCK
    validity = (block_ids < live_blocks[owner]).astype(jnp.float32)
    landmark = ((owner // KF_GROUPS) * (KF_GROUPS * LDEV) + obs_landmark).astype(jnp.int32)
    sol_land = jnp.zeros_like(land_rhs)
    sol_key = jnp.zeros_like(key_rhs)
    res_land, res_key = land_rhs, key_rhs
    dir_land, dir_key = land_rhs, key_rhs
    norm_now = jnp.sum(res_land * res_land) + jnp.sum(res_key * res_key)
    for iteration in range(ITERS):
        prod_land, prod_key = normal_product(dir_land, dir_key, land_jac, key_jac, landmark, obs_keyframe, validity, preint, land_damp, key_damp)
        step_size = norm_now / (jnp.sum(dir_land * prod_land) + jnp.sum(dir_key * prod_key))
        sol_land = sol_land + step_size * dir_land
        sol_key = sol_key + step_size * dir_key
        res_land = res_land - step_size * prod_land
        res_key = res_key - step_size * prod_key
        norm_next = jnp.sum(res_land * res_land) + jnp.sum(res_key * res_key)
        dir_land = res_land + (norm_next / norm_now) * dir_land
        dir_key = res_key + (norm_next / norm_now) * dir_key
        norm_now = norm_next
    return sol_land, sol_key
```

```python
import functools

import jax
import jax.numpy as jnp
from jax import lax
from jax.experimental import pallas as pl
from jax.experimental.pallas import tpu as pltpu
from jax.sharding import Mesh
from jax.sharding import PartitionSpec as P

WSTATES = 16
SDIM = 15
BLOCK = 128
ITERS = 2
WPAR = 240
LOW = 256
CHUNK = 1024
KF = ("kf_0", "kf_1")
LM = ("lm_0", "lm_1")
LM_KF = ("lm_0", "lm_1", "kf_0", "kf_1")


def window_product(preint, vectors):
    windows = preint.shape[1] // WPAR
    blocks = preint.reshape(WPAR, windows, WPAR)
    stacked = vectors.reshape(SDIM, windows, WSTATES).transpose(1, 2, 0).reshape(windows, WPAR)
    mapped = jnp.einsum("awb,wb->wa", blocks, stacked, precision=lax.Precision.HIGHEST)
    return (
        mapped.reshape(windows, WSTATES, SDIM).transpose(2, 0, 1).reshape(SDIM, windows * WSTATES)
    )


def split_parts(value):
    high = value.astype(jnp.bfloat16)
    low = (value - high.astype(jnp.float32)).astype(jnp.bfloat16)
    return high, low


def table_parts(full):
    channels, extent = full.shape
    folded = full.reshape(channels * (extent // LOW), LOW)
    high = lax.reduce_precision(folded, exponent_bits=8, mantissa_bits=7)
    return high.astype(jnp.bfloat16), (folded - high).astype(jnp.bfloat16)


def observe_kernel(
    valid_ref, lpos_ref, kpos_ref, ljac_ref, kjac_ref,
    lhi_ref, llo_ref, khi_ref, klo_ref,
    lacc_ref, kacc_ref,
):
    step = pl.program_id(0)

    @pl.when(step == 0)
    def _():
        lacc_ref[...] = jnp.zeros_like(lacc_ref)
        kacc_ref[...] = jnp.zeros_like(kacc_ref)

    span = valid_ref.shape[1]
    land_high = lhi_ref.shape[0] // 3
    key_high = khi_ref.shape[0] // SDIM
    lpos = lpos_ref[...]
    kpos = kpos_ref[...]
    land_hot = (
        lax.broadcasted_iota(jnp.int32, (LOW, span), 0) == lpos % LOW
    ).astype(jnp.bfloat16)
    key_hot = (
        lax.broadcasted_iota(jnp.int32, (LOW, span), 0) == kpos % LOW
    ).astype(jnp.bfloat16)
    land_sel = (
        lax.broadcasted_iota(jnp.int32, (land_high, span), 0) == lpos // LOW
    ).astype(jnp.float32)
    key_sel = (
        lax.broadcasted_iota(jnp.int32, (key_high, span), 0) == kpos // LOW
    ).astype(jnp.float32)

    def gather(hi_ref, lo_ref, hot, sel, channels, high):
        rows = jnp.dot(hi_ref[...], hot, preferred_element_type=jnp.float32) + jnp.dot(
            lo_ref[...], hot, preferred_element_type=jnp.float32
        )
        return [
            jnp.sum(rows[c * high:(c + 1) * high, :] * sel, axis=0, keepdims=True)
            for c in range(channels)
        ]

    seen_land = gather(lhi_ref, llo_ref, land_hot, land_sel, 3, land_high)
    seen_key = gather(khi_ref, klo_ref, key_hot, key_sel, SDIM, key_high)
    ljac = ljac_ref[...]
    kjac = kjac_ref[...]
    valid = valid_ref[...]
    image = []
    for r in range(2):
        total = ljac[r * 3:r * 3 + 1, :] * seen_land[0]
        for c in range(1, 3):
            total = total + ljac[r * 3 + c:r * 3 + c + 1, :] * seen_land[c]
        for c in range(SDIM):
            total = total + kjac[r * SDIM + c:r * SDIM + c + 1, :] * seen_key[c]
        image.append(total * valid)

    def scatter(acc_ref, jac, channels, hot, sel):
        placed = jnp.concatenate(
            [
                (jac[c:c + 1, :] * image[0] + jac[channels + c:channels + c + 1, :] * image[1])
                * sel
                for c in range(channels)
            ],
            axis=0,
        )
        high, low = split_parts(placed)
        dims = (((1,), (1,)), ((), ()))
        acc_ref[...] += lax.dot_general(
            high, hot, dims, preferred_element_type=jnp.float32
        ) + lax.dot_general(low, hot, dims, preferred_element_type=jnp.float32)

    scatter(lacc_ref, ljac, 3, land_hot, land_sel)
    scatter(kacc_ref, kjac, SDIM, key_hot, key_sel)


def observe(valid, land_pos, key_pos, land_jac, key_jac, land_full, key_full):
    count = land_jac.shape[1]
    lhi, llo = table_parts(land_full)
    khi, klo = table_parts(key_full)
    row = lambda i: (0, i)
    whole = lambda i: (0, 0)
    lacc, kacc = pl.pallas_call(
        observe_kernel,
        grid=(count // CHUNK,),
        in_specs=[
            pl.BlockSpec((1, CHUNK), row),
            pl.BlockSpec((1, CHUNK), row),
            pl.BlockSpec((1, CHUNK), row),
            pl.BlockSpec((land_jac.shape[0], CHUNK), row),
            pl.BlockSpec((key_jac.shape[0], CHUNK), row),
            pl.BlockSpec(lhi.shape, whole),
            pl.BlockSpec(llo.shape, whole),
            pl.BlockSpec(khi.shape, whole),
            pl.BlockSpec(klo.shape, whole),
        ],
        out_specs=[
            pl.BlockSpec((lhi.shape[0], LOW), whole),
            pl.BlockSpec((khi.shape[0], LOW), whole),
        ],
        out_shape=[
            jax.ShapeDtypeStruct((lhi.shape[0], LOW), jnp.float32),
            jax.ShapeDtypeStruct((khi.shape[0], LOW), jnp.float32),
        ],
        compiler_params=pltpu.CompilerParams(dimension_semantics=("arbitrary",)),
    )(valid, land_pos, key_pos, land_jac, key_jac, lhi, llo, khi, klo)
    return lacc.reshape(land_full.shape), kacc.reshape(key_full.shape)


def shards(
    land_rhs,
    key_rhs,
    land_damp,
    key_damp,
    land_jac,
    key_jac,
    obs_landmark,
    obs_keyframe,
    live_blocks,
    preint,
):
    state_dev = key_rhs.shape[1]
    kf_count = lax.axis_size(KF)
    count = obs_landmark.shape[0]
    owner_block = obs_keyframe // state_dev
    key_pos = (owner_block // kf_count * state_dev + obs_keyframe % state_dev).reshape(1, count)
    land_pos = obs_landmark.reshape(1, count)
    live = live_blocks[0]
    valid = (jnp.arange(count, dtype=jnp.int32) // BLOCK < live).astype(jnp.float32).reshape(1, count)

    def normal_product(dir_land, dir_key):
        land_full = lax.all_gather(dir_land, KF, axis=1, tiled=True)
        key_full = lax.all_gather(dir_key, LM, axis=1, tiled=True)
        summed_land, summed_key = observe(
            valid, land_pos, key_pos, land_jac, key_jac, land_full, key_full
        )
        prod_land = lax.psum_scatter(summed_land, KF, scatter_dimension=1, tiled=True) + (
            land_damp * dir_land
        )
        prod_key = (
            lax.psum_scatter(summed_key, LM, scatter_dimension=1, tiled=True)
            + key_damp * dir_key
            + window_product(preint, dir_key)
        )
        return (prod_land, prod_key)

    def both_products(part_land, part_key, image_land, image_key):
        local = jnp.stack(
            [
                jnp.sum(part_land * part_land) + jnp.sum(part_key * part_key),
                jnp.sum(part_land * image_land) + jnp.sum(part_key * image_key),
            ]
        )
        total = lax.psum(local, LM_KF)
        return total[0], total[1]

    res_key = key_rhs
    res_land = land_rhs
    sol_land = jnp.zeros_like(res_land)
    sol_key = jnp.zeros_like(res_key)

    image_land, image_key = normal_product(res_land, res_key)
    norm_now, product = both_products(res_land, res_key, image_land, image_key)
    step_size = norm_now / product
    dir_land, dir_key = (res_land, res_key)
    along_land, along_key = (image_land, image_key)
    for iteration in range(ITERS):
        sol_land = sol_land + step_size * dir_land
        sol_key = sol_key + step_size * dir_key
        res_land = res_land - step_size * along_land
        res_key = res_key - step_size * along_key
        if iteration + 1 < ITERS:
            image_land, image_key = normal_product(res_land, res_key)
            norm_next, product = both_products(res_land, res_key, image_land, image_key)
            beta_ratio = norm_next / norm_now
            step_size = norm_next / (product - beta_ratio * norm_next / step_size)
            dir_land = res_land + beta_ratio * dir_land
            dir_key = res_key + beta_ratio * dir_key
            along_land = image_land + beta_ratio * along_land
            along_key = image_key + beta_ratio * along_key
            norm_now = norm_next
    return (sol_land, sol_key)


def solution(mesh):
    split = Mesh(mesh.devices.reshape(4, 4, 4, 2), ("lm_0", "lm_1", "kf_0", "kf_1"))
    in_specs = (
        P(None, LM_KF),
        P(None, LM_KF),
        P(None, LM_KF),
        P(None, LM_KF),
        P(None, LM_KF),
        P(None, LM_KF),
        P(LM_KF),
        P(LM_KF),
        P(LM_KF),
        P(None, LM_KF),
    )
    out_specs = (P(None, LM_KF), P(None, LM_KF))
    return jax.shard_map(
        shards, mesh=split, in_specs=in_specs, out_specs=out_specs, check_vma=False
    )
```

```python
import functools

import jax
import jax.numpy as jnp
from jax import lax
from jax.experimental import pallas as pl
from jax.experimental.pallas import tpu as pltpu
from jax.sharding import Mesh
from jax.sharding import PartitionSpec as P

WSTATES = 16
SDIM = 15
BLOCK = 128
ITERS = 2
WPAR = 240
LOW = 256
CHUNK = 1024
KF = ("kf_0", "kf_1")
LM = ("lm_0", "lm_1")
LM_KF = ("lm_0", "lm_1", "kf_0", "kf_1")


def window_product(preint, vectors):
    windows = preint.shape[1] // WPAR
    blocks = preint.reshape(WPAR, windows, WPAR)
    stacked = vectors.reshape(SDIM, windows, WSTATES).transpose(1, 2, 0).reshape(windows, WPAR)
    mapped = jnp.einsum("awb,wb->wa", blocks, stacked, precision=lax.Precision.HIGHEST)
    return (
        mapped.reshape(windows, WSTATES, SDIM).transpose(2, 0, 1).reshape(SDIM, windows * WSTATES)
    )


def split_parts(value):
    high = value.astype(jnp.bfloat16)
    low = (value - high.astype(jnp.float32)).astype(jnp.bfloat16)
    return high, low


def table_parts(full):
    channels, extent = full.shape
    folded = full.reshape(channels * (extent // LOW), LOW)
    high = lax.reduce_precision(folded, exponent_bits=8, mantissa_bits=7)
    return high.astype(jnp.bfloat16), (folded - high).astype(jnp.bfloat16)


def in_order(blocks, dim):
    shape = list(blocks.shape[1:])
    shape[dim] *= blocks.shape[0]
    return jnp.moveaxis(blocks, 0, dim).reshape(shape)


def from_everyone(value, axis):
    copies = jnp.broadcast_to(value, (lax.axis_size(axis), *value.shape))
    return lax.all_to_all(copies, axis, split_axis=0, concat_axis=0, tiled=True)


def gather_directly(value, axis, dim):
    return in_order(from_everyone(value, axis), dim)


def split_up(value, dim, devices):
    before, after = (value.shape[:dim], value.shape[dim + 1 :])
    return jnp.moveaxis(value.reshape(*before, devices, -1, *after), dim, 0)


def sum_at_owner(value, axis, dim):
    blocks = split_up(value, dim, lax.axis_size(axis))
    arrived = lax.all_to_all(blocks, axis, split_axis=0, concat_axis=0, tiled=True)
    return arrived.sum(axis=0)


def make_observe_kernel(with_scatter):
    def kernel(valid_ref, lpos_ref, kpos_ref, ljac_ref, kjac_ref, lhi_ref, llo_ref, khi_ref, klo_ref, *outs):
        if with_scatter:
            sq_ref, lacc_ref, kacc_ref = outs
        else:
            (sq_ref,) = outs
        step = pl.program_id(0)

        @pl.when(step == 0)
        def _():
            for ref in outs:
                ref[...] = jnp.zeros_like(ref)

        span = valid_ref.shape[1]
        land_high = lhi_ref.shape[0] // 3
        key_high = khi_ref.shape[0] // SDIM
        lpos = lpos_ref[...]
        kpos = kpos_ref[...]
        land_hot = (
            lax.broadcasted_iota(jnp.int32, (LOW, span), 0) == lpos % LOW
        ).astype(jnp.bfloat16)
        key_hot = (
            lax.broadcasted_iota(jnp.int32, (LOW, span), 0) == kpos % LOW
        ).astype(jnp.bfloat16)
        land_sel = (
            lax.broadcasted_iota(jnp.int32, (land_high, span), 0) == lpos // LOW
        ).astype(jnp.float32)
        key_sel = (
            lax.broadcasted_iota(jnp.int32, (key_high, span), 0) == kpos // LOW
        ).astype(jnp.float32)

        def gather(hi_ref, lo_ref, hot, sel, channels, high):
            rows = jnp.dot(hi_ref[...], hot, preferred_element_type=jnp.float32) + jnp.dot(
                lo_ref[...], hot, preferred_element_type=jnp.float32
            )
            return [
                jnp.sum(rows[c * high:(c + 1) * high, :] * sel, axis=0, keepdims=True)
                for c in range(channels)
            ]

        seen_land = gather(lhi_ref, llo_ref, land_hot, land_sel, 3, land_high)
        seen_key = gather(khi_ref, klo_ref, key_hot, key_sel, SDIM, key_high)
        ljac = ljac_ref[...]
        kjac = kjac_ref[...]
        valid = valid_ref[...]
        image = []
        for r in range(2):
            total = ljac[r * 3:r * 3 + 1, :] * seen_land[0]
            for c in range(1, 3):
                total = total + ljac[r * 3 + c:r * 3 + c + 1, :] * seen_land[c]
            for c in range(SDIM):
                total = total + kjac[r * SDIM + c:r * SDIM + c + 1, :] * seen_key[c]
            image.append(total * valid)
        sq_ref[...] += image[0] * image[0] + image[1] * image[1]
        if not with_scatter:
            return

        def scatter(acc_ref, jac, channels, hot, sel):
            placed = jnp.concatenate(
                [
                    (jac[c:c + 1, :] * image[0] + jac[channels + c:channels + c + 1, :] * image[1])
                    * sel
                    for c in range(channels)
                ],
                axis=0,
            )
            high, low = split_parts(placed)
            dims = (((1,), (1,)), ((), ()))
            acc_ref[...] += lax.dot_general(
                high, hot, dims, preferred_element_type=jnp.float32
            ) + lax.dot_general(low, hot, dims, preferred_element_type=jnp.float32)

        scatter(lacc_ref, ljac, 3, land_hot, land_sel)
        scatter(kacc_ref, kjac, SDIM, key_hot, key_sel)

    return kernel


def observe(valid, land_pos, key_pos, land_jac, key_jac, land_full, key_full, with_scatter):
    count = land_jac.shape[1]
    lhi, llo = table_parts(land_full)
    khi, klo = table_parts(key_full)
    row = lambda i: (0, i)
    whole = lambda i: (0, 0)
    out_specs = [pl.BlockSpec((1, CHUNK), whole)]
    out_shape = [jax.ShapeDtypeStruct((1, CHUNK), jnp.float32)]
    if with_scatter:
        out_specs += [
            pl.BlockSpec((lhi.shape[0], LOW), whole),
            pl.BlockSpec((khi.shape[0], LOW), whole),
        ]
        out_shape += [
            jax.ShapeDtypeStruct((lhi.shape[0], LOW), jnp.float32),
            jax.ShapeDtypeStruct((khi.shape[0], LOW), jnp.float32),
        ]
    outs = pl.pallas_call(
        make_observe_kernel(with_scatter),
        grid=(count // CHUNK,),
        in_specs=[
            pl.BlockSpec((1, CHUNK), row),
            pl.BlockSpec((1, CHUNK), row),
            pl.BlockSpec((1, CHUNK), row),
            pl.BlockSpec((land_jac.shape[0], CHUNK), row),
            pl.BlockSpec((key_jac.shape[0], CHUNK), row),
            pl.BlockSpec(lhi.shape, whole),
            pl.BlockSpec(llo.shape, whole),
            pl.BlockSpec(khi.shape, whole),
            pl.BlockSpec(klo.shape, whole),
        ],
        out_specs=out_specs,
        out_shape=out_shape,
        compiler_params=pltpu.CompilerParams(dimension_semantics=("arbitrary",)),
    )(valid, land_pos, key_pos, land_jac, key_jac, lhi, llo, khi, klo)
    if not with_scatter:
        return jnp.sum(outs[0]), None, None
    sq, lacc, kacc = outs
    return jnp.sum(sq), lacc.reshape(land_full.shape), kacc.reshape(key_full.shape)


def shards(
    land_rhs,
    key_rhs,
    land_damp,
    key_damp,
    land_jac,
    key_jac,
    obs_landmark,
    obs_keyframe,
    live_blocks,
    preint,
):
    state_dev = key_rhs.shape[1]
    kf_count = lax.axis_size(KF)
    count = obs_landmark.shape[0]
    owner_block = obs_keyframe // state_dev
    key_pos = (owner_block // kf_count * state_dev + obs_keyframe % state_dev).reshape(1, count)
    land_pos = obs_landmark.reshape(1, count)
    live = live_blocks[0]
    valid = (jnp.arange(count, dtype=jnp.int32) // BLOCK < live).astype(jnp.float32).reshape(1, count)

    def reduce_all(values):
        return from_everyone(jnp.stack(values), LM_KF).sum(axis=0)

    def image_norms(dir_land, dir_key, with_scatter):
        land_full = gather_directly(dir_land, KF, 1)
        key_full = gather_directly(dir_key, LM, 1)
        squared, summed_land, summed_key = observe(
            valid, land_pos, key_pos, land_jac, key_jac, land_full, key_full, with_scatter
        )
        windowed = window_product(preint, dir_key)
        local_rr = jnp.sum(dir_land * dir_land) + jnp.sum(dir_key * dir_key)
        local_product = (
            squared
            + jnp.sum(land_damp * dir_land * dir_land)
            + jnp.sum(dir_key * (key_damp * dir_key + windowed))
        )
        rr, product = reduce_all([local_rr, local_product])
        if not with_scatter:
            return rr, product, None, None
        prod_land = sum_at_owner(summed_land, KF, 1) + land_damp * dir_land
        prod_key = sum_at_owner(summed_key, LM, 1) + key_damp * dir_key + windowed
        return rr, product, prod_land, prod_key

    res_land, res_key = land_rhs, key_rhs
    norm_now, product, along_land, along_key = image_norms(res_land, res_key, True)
    step_size = norm_now / product
    sol_land = step_size * res_land
    sol_key = step_size * res_key
    dir_land, dir_key = res_land, res_key
    res_land = res_land - step_size * along_land
    res_key = res_key - step_size * along_key
    norm_next, product, _, _ = image_norms(res_land, res_key, False)
    beta_ratio = norm_next / norm_now
    step_size = norm_next / (product - beta_ratio * norm_next / step_size)
    dir_land = res_land + beta_ratio * dir_land
    dir_key = res_key + beta_ratio * dir_key
    sol_land = sol_land + step_size * dir_land
    sol_key = sol_key + step_size * dir_key
    return (sol_land, sol_key)


def solution(mesh):
    split = Mesh(mesh.devices.reshape(4, 4, 4, 2), ("lm_0", "lm_1", "kf_0", "kf_1"))
    in_specs = (
        P(None, LM_KF),
        P(None, LM_KF),
        P(None, LM_KF),
        P(None, LM_KF),
        P(None, LM_KF),
        P(None, LM_KF),
        P(LM_KF),
        P(LM_KF),
        P(LM_KF),
        P(None, LM_KF),
    )
    out_specs = (P(None, LM_KF), P(None, LM_KF))
    return jax.shard_map(
        shards, mesh=split, in_specs=in_specs, out_specs=out_specs, check_vma=False
    )
```

```python
import functools

import jax
import jax.numpy as jnp
from jax import lax
from jax.experimental import pallas as pl
from jax.experimental.pallas import tpu as pltpu
from jax.sharding import Mesh
from jax.sharding import PartitionSpec as P

WSTATES = 16
SDIM = 15
BLOCK = 128
ITERS = 2
WPAR = 240
LOW = 256
CHUNK = 2048
KF = ("kf_0", "kf_1")
LM = ("lm_0", "lm_1")
LM_KF = ("lm_0", "lm_1", "kf_0", "kf_1")


def window_product(preint, vectors):
    windows = preint.shape[1] // WPAR
    stacked = vectors.reshape(SDIM, windows, WSTATES).transpose(1, 2, 0).reshape(windows * WPAR)
    owner = jnp.arange(windows * WPAR, dtype=jnp.int32) // WPAR
    spread = jnp.where(
        owner[:, None] == jnp.arange(windows, dtype=jnp.int32)[None, :], stacked[:, None], 0.0
    )
    mapped = jnp.dot(preint, spread, precision=lax.Precision.HIGHEST)
    return (
        mapped.reshape(WSTATES, SDIM, windows).transpose(1, 2, 0).reshape(SDIM, windows * WSTATES)
    )


def split_parts(value):
    high = value.astype(jnp.bfloat16)
    low = (value - high.astype(jnp.float32)).astype(jnp.bfloat16)
    return high, low


def table_parts(full):
    channels, extent = full.shape
    folded = full.reshape(channels * (extent // LOW), LOW)
    high = lax.reduce_precision(folded, exponent_bits=8, mantissa_bits=7)
    return jnp.concatenate(
        [high.astype(jnp.bfloat16), (folded - high).astype(jnp.bfloat16)], axis=1
    )


def in_order(blocks, dim):
    shape = list(blocks.shape[1:])
    shape[dim] *= blocks.shape[0]
    return jnp.moveaxis(blocks, 0, dim).reshape(shape)


def from_everyone(value, axis):
    copies = jnp.broadcast_to(value, (lax.axis_size(axis), *value.shape))
    return lax.all_to_all(copies, axis, split_axis=0, concat_axis=0, tiled=True)


def gather_directly(value, axis, dim):
    return in_order(from_everyone(value, axis), dim)


def split_up(value, dim, devices):
    before, after = (value.shape[:dim], value.shape[dim + 1 :])
    return jnp.moveaxis(value.reshape(*before, devices, -1, *after), dim, 0)


def sum_at_owner(value, axis, dim):
    blocks = split_up(value, dim, lax.axis_size(axis))
    arrived = lax.all_to_all(blocks, axis, split_axis=0, concat_axis=0, tiled=True)
    return arrived.sum(axis=0)


def sum_at_owner_with(value, scalars, axis):
    devices = lax.axis_size(axis)
    blocks = split_up(value, 1, devices)
    extra = jnp.zeros((devices, 1, blocks.shape[2]), jnp.float32)
    extra = extra.at[:, 0, : scalars.shape[0]].set(scalars[None, :])
    blocks = jnp.concatenate([blocks, extra], axis=1)
    arrived = lax.all_to_all(blocks, axis, split_axis=0, concat_axis=0, tiled=True).sum(axis=0)
    return arrived[:-1], arrived[-1, : scalars.shape[0]]


def make_observe_kernel(with_scatter):
    def kernel(valid_ref, lpos_ref, kpos_ref, ljac_ref, kjac_ref, ltab_ref, ktab_ref, *outs):
        if with_scatter:
            sq_ref, lacc_ref, kacc_ref = outs
        else:
            (sq_ref,) = outs
        step = pl.program_id(0)

        @pl.when(step == 0)
        def _():
            for ref in outs:
                ref[...] = jnp.zeros_like(ref)

        span = valid_ref.shape[1]
        land_high = ltab_ref.shape[0] // 3
        key_high = ktab_ref.shape[0] // SDIM
        lpos = lpos_ref[...]
        kpos = kpos_ref[...]
        land_hot = (
            lax.broadcasted_iota(jnp.int32, (LOW, span), 0) == lpos % LOW
        ).astype(jnp.bfloat16)
        key_hot = (
            lax.broadcasted_iota(jnp.int32, (LOW, span), 0) == kpos % LOW
        ).astype(jnp.bfloat16)
        land_sel = (
            lax.broadcasted_iota(jnp.int32, (land_high, span), 0) == lpos // LOW
        ).astype(jnp.float32)
        key_sel = (
            lax.broadcasted_iota(jnp.int32, (key_high, span), 0) == kpos // LOW
        ).astype(jnp.float32)

        def gather(tab_ref, hot, sel, channels, high):
            rows = jnp.dot(
                tab_ref[...], jnp.concatenate([hot, hot], axis=0),
                preferred_element_type=jnp.float32,
            )
            return [
                jnp.sum(rows[c * high:(c + 1) * high, :] * sel, axis=0, keepdims=True)
                for c in range(channels)
            ]

        seen_land = gather(ltab_ref, land_hot, land_sel, 3, land_high)
        seen_key = gather(ktab_ref, key_hot, key_sel, SDIM, key_high)
        ljac = ljac_ref[...]
        kjac = kjac_ref[...]
        valid = valid_ref[...]
        image = []
        for r in range(2):
            total = ljac[r * 3:r * 3 + 1, :] * seen_land[0]
            for c in range(1, 3):
                total = total + ljac[r * 3 + c:r * 3 + c + 1, :] * seen_land[c]
            for c in range(SDIM):
                total = total + kjac[r * SDIM + c:r * SDIM + c + 1, :] * seen_key[c]
            image.append(total * valid)
        sq_ref[...] += image[0] * image[0] + image[1] * image[1]
        if not with_scatter:
            return

        def scatter(acc_ref, jac, channels, hot, sel):
            placed = jnp.concatenate(
                [
                    (jac[c:c + 1, :] * image[0] + jac[channels + c:channels + c + 1, :] * image[1])
                    * sel
                    for c in range(channels)
                ],
                axis=0,
            )
            high, low = split_parts(placed)
            dims = (((1,), (1,)), ((), ()))
            acc_ref[...] += lax.dot_general(
                high, hot, dims, preferred_element_type=jnp.float32
            ) + lax.dot_general(low, hot, dims, preferred_element_type=jnp.float32)

        scatter(lacc_ref, ljac, 3, land_hot, land_sel)
        scatter(kacc_ref, kjac, SDIM, key_hot, key_sel)

    return kernel


def observe(valid, land_pos, key_pos, land_jac, key_jac, land_full, key_full, with_scatter):
    count = land_jac.shape[1]
    ltab = table_parts(land_full)
    ktab = table_parts(key_full)
    row = lambda i: (0, i)
    whole = lambda i: (0, 0)
    out_specs = [pl.BlockSpec((1, CHUNK), whole)]
    out_shape = [jax.ShapeDtypeStruct((1, CHUNK), jnp.float32)]
    if with_scatter:
        out_specs += [
            pl.BlockSpec((ltab.shape[0], LOW), whole),
            pl.BlockSpec((ktab.shape[0], LOW), whole),
        ]
        out_shape += [
            jax.ShapeDtypeStruct((ltab.shape[0], LOW), jnp.float32),
            jax.ShapeDtypeStruct((ktab.shape[0], LOW), jnp.float32),
        ]
    outs = pl.pallas_call(
        make_observe_kernel(with_scatter),
        grid=(count // CHUNK,),
        in_specs=[
            pl.BlockSpec((1, CHUNK), row),
            pl.BlockSpec((1, CHUNK), row),
            pl.BlockSpec((1, CHUNK), row),
            pl.BlockSpec((land_jac.shape[0], CHUNK), row),
            pl.BlockSpec((key_jac.shape[0], CHUNK), row),
            pl.BlockSpec(ltab.shape, whole),
            pl.BlockSpec(ktab.shape, whole),
        ],
        out_specs=out_specs,
        out_shape=out_shape,
        compiler_params=pltpu.CompilerParams(dimension_semantics=("arbitrary",)),
    )(valid, land_pos, key_pos, land_jac, key_jac, ltab, ktab)
    if not with_scatter:
        return jnp.sum(outs[0]), None, None
    sq, lacc, kacc = outs
    return jnp.sum(sq), lacc.reshape(land_full.shape), kacc.reshape(key_full.shape)


def shards(
    land_rhs,
    key_rhs,
    land_damp,
    key_damp,
    land_jac,
    key_jac,
    obs_landmark,
    obs_keyframe,
    live_blocks,
    preint,
):
    state_dev = key_rhs.shape[1]
    kf_count = lax.axis_size(KF)
    count = obs_landmark.shape[0]
    owner_block = obs_keyframe // state_dev
    key_pos = (owner_block // kf_count * state_dev + obs_keyframe % state_dev).reshape(1, count)
    land_pos = obs_landmark.reshape(1, count)
    live = live_blocks[0]
    valid = (jnp.arange(count, dtype=jnp.int32) // BLOCK < live).astype(jnp.float32).reshape(1, count)

    def reduce_all(values):
        return from_everyone(jnp.stack(values), LM_KF).sum(axis=0)

    def image_norms(dir_land, dir_key, with_scatter):
        land_full = gather_directly(dir_land, KF, 1)
        key_full = gather_directly(dir_key, LM, 1)
        squared, summed_land, summed_key = observe(
            valid, land_pos, key_pos, land_jac, key_jac, land_full, key_full, with_scatter
        )
        windowed = window_product(preint, dir_key)
        local_rr = jnp.sum(dir_land * dir_land) + jnp.sum(dir_key * dir_key)
        local_product = (
            squared
            + jnp.sum(land_damp * dir_land * dir_land)
            + jnp.sum(dir_key * (key_damp * dir_key + windowed))
        )
        if not with_scatter:
            rr, product = reduce_all([local_rr, local_product])
            return rr, product, None, None
        owned_land, partial = sum_at_owner_with(
            summed_land, jnp.stack([local_rr, local_product]), KF
        )
        owned_key, total = sum_at_owner_with(summed_key, partial, LM)
        prod_land = owned_land + land_damp * dir_land
        prod_key = owned_key + key_damp * dir_key + windowed
        return total[0], total[1], prod_land, prod_key

    res_land, res_key = land_rhs, key_rhs
    norm_now, product, along_land, along_key = image_norms(res_land, res_key, True)
    step_size = norm_now / product
    sol_land = step_size * res_land
    sol_key = step_size * res_key
    dir_land, dir_key = res_land, res_key
    res_land = res_land - step_size * along_land
    res_key = res_key - step_size * along_key
    norm_next, product, _, _ = image_norms(res_land, res_key, False)
    beta_ratio = norm_next / norm_now
    step_size = norm_next / (product - beta_ratio * norm_next / step_size)
    dir_land = res_land + beta_ratio * dir_land
    dir_key = res_key + beta_ratio * dir_key
    sol_land = sol_land + step_size * dir_land
    sol_key = sol_key + step_size * dir_key
    return (sol_land, sol_key)


def solution(mesh):
    split = Mesh(mesh.devices.reshape(4, 4, 4, 2), ("lm_0", "lm_1", "kf_0", "kf_1"))
    in_specs = (
        P(None, LM_KF),
        P(None, LM_KF),
        P(None, LM_KF),
        P(None, LM_KF),
        P(None, LM_KF),
        P(None, LM_KF),
        P(LM_KF),
        P(LM_KF),
        P(LM_KF),
        P(None, LM_KF),
    )
    out_specs = (P(None, LM_KF), P(None, LM_KF))
    return jax.shard_map(
        shards, mesh=split, in_specs=in_specs, out_specs=out_specs, check_vma=False
    )
```

```python
import functools

import jax
import jax.numpy as jnp
from jax import lax
from jax.experimental import pallas as pl
from jax.experimental.pallas import tpu as pltpu
from jax.sharding import Mesh
from jax.sharding import PartitionSpec as P

WSTATES = 16
SDIM = 15
BLOCK = 128
ITERS = 2
WPAR = 240
LOW = 256
CHUNK = 2048
KF = ("kf_0", "kf_1")
LM = ("lm_0", "lm_1")
LM_KF = ("lm_0", "lm_1", "kf_0", "kf_1")


def window_product(preint, vectors):
    windows = preint.shape[1] // WPAR
    stacked = vectors.reshape(SDIM, windows, WSTATES).transpose(1, 2, 0).reshape(windows * WPAR)
    owner = jnp.arange(windows * WPAR, dtype=jnp.int32) // WPAR
    spread = jnp.where(
        owner[:, None] == jnp.arange(windows, dtype=jnp.int32)[None, :], stacked[:, None], 0.0
    )
    mapped = jnp.dot(preint, spread, precision=lax.Precision.HIGHEST)
    return (
        mapped.reshape(WSTATES, SDIM, windows).transpose(1, 2, 0).reshape(SDIM, windows * WSTATES)
    )


def split_parts(value):
    high = value.astype(jnp.bfloat16)
    low = (value - high.astype(jnp.float32)).astype(jnp.bfloat16)
    return high, low


def table_parts(full):
    channels, extent = full.shape
    folded = full.reshape(channels * (extent // LOW), LOW)
    high = lax.reduce_precision(folded, exponent_bits=8, mantissa_bits=7)
    return jnp.concatenate(
        [high.astype(jnp.bfloat16), (folded - high).astype(jnp.bfloat16)], axis=1
    )


def in_order(blocks, dim):
    shape = list(blocks.shape[1:])
    shape[dim] *= blocks.shape[0]
    return jnp.moveaxis(blocks, 0, dim).reshape(shape)


def from_everyone(value, axis):
    copies = jnp.broadcast_to(value, (lax.axis_size(axis), *value.shape))
    return lax.all_to_all(copies, axis, split_axis=0, concat_axis=0, tiled=True)


def gather_directly(value, axis, dim):
    return in_order(from_everyone(value, axis), dim)


def split_up(value, dim, devices):
    before, after = (value.shape[:dim], value.shape[dim + 1 :])
    return jnp.moveaxis(value.reshape(*before, devices, -1, *after), dim, 0)


def sum_at_owner(value, axis, dim):
    blocks = split_up(value, dim, lax.axis_size(axis))
    arrived = lax.all_to_all(blocks, axis, split_axis=0, concat_axis=0, tiled=True)
    return arrived.sum(axis=0)


def sum_at_owner_with(value, scalars, axis):
    devices = lax.axis_size(axis)
    blocks = split_up(value, 1, devices)
    extra = jnp.zeros((devices, 1, blocks.shape[2]), jnp.float32)
    extra = extra.at[:, 0, : scalars.shape[0]].set(scalars[None, :])
    blocks = jnp.concatenate([blocks, extra], axis=1)
    arrived = lax.all_to_all(blocks, axis, split_axis=0, concat_axis=0, tiled=True).sum(axis=0)
    return arrived[:-1], arrived[-1, : scalars.shape[0]]


def shifted_gather(value, axis):
    devices = lax.axis_size(axis)
    pieces = [value] + [
        lax.ppermute(value, axis, [(i, (i + k) % devices) for i in range(devices)])
        for k in range(1, devices)
    ]
    return jnp.concatenate(pieces, axis=1)


def shifted_sum_with(value, scalars, axis):
    devices = lax.axis_size(axis)
    width = value.shape[1] // devices
    extra = jnp.zeros((1, width), jnp.float32).at[0, : scalars.shape[0]].set(scalars)
    total = value[:, :width]
    arrived = [extra]
    for k in range(1, devices):
        block = jnp.concatenate([value[:, k * width:(k + 1) * width], extra], axis=0)
        moved = lax.ppermute(block, axis, [(i, (i - k) % devices) for i in range(devices)])
        total = total + moved[:-1]
        arrived.append(moved[-1:])
    me = lax.axis_index(axis)
    by_shift = jnp.concatenate(arrived, axis=0)[:, : scalars.shape[0]]
    by_source = jnp.take(by_shift, (jnp.arange(devices) - me) % devices, axis=0)
    return total, jnp.sum(by_source, axis=0)


def make_observe_kernel(with_scatter):
    def kernel(valid_ref, lpos_ref, kpos_ref, ljac_ref, kjac_ref, ltab_ref, ktab_ref, *outs):
        if with_scatter:
            sq_ref, lacc_ref, kacc_ref = outs
        else:
            (sq_ref,) = outs
        step = pl.program_id(0)

        @pl.when(step == 0)
        def _():
            for ref in outs:
                ref[...] = jnp.zeros_like(ref)

        span = valid_ref.shape[1]
        land_high = ltab_ref.shape[0] // 3
        key_high = ktab_ref.shape[0] // SDIM
        lpos = lpos_ref[...]
        kpos = kpos_ref[...]
        land_hot = (
            lax.broadcasted_iota(jnp.int32, (LOW, span), 0) == lpos % LOW
        ).astype(jnp.bfloat16)
        key_hot = (
            lax.broadcasted_iota(jnp.int32, (LOW, span), 0) == kpos % LOW
        ).astype(jnp.bfloat16)
        land_sel = (
            lax.broadcasted_iota(jnp.int32, (land_high, span), 0) == lpos // LOW
        ).astype(jnp.float32)
        key_sel = (
            lax.broadcasted_iota(jnp.int32, (key_high, span), 0) == kpos // LOW
        ).astype(jnp.float32)

        def gather(tab_ref, hot, sel, channels, high):
            rows = jnp.dot(
                tab_ref[...], jnp.concatenate([hot, hot], axis=0),
                preferred_element_type=jnp.float32,
            )
            return [
                jnp.sum(rows[c * high:(c + 1) * high, :] * sel, axis=0, keepdims=True)
                for c in range(channels)
            ]

        seen_land = gather(ltab_ref, land_hot, land_sel, 3, land_high)
        seen_key = gather(ktab_ref, key_hot, key_sel, SDIM, key_high)
        ljac = ljac_ref[...]
        kjac = kjac_ref[...]
        valid = valid_ref[...]
        image = []
        for r in range(2):
            total = ljac[r * 3:r * 3 + 1, :] * seen_land[0]
            for c in range(1, 3):
                total = total + ljac[r * 3 + c:r * 3 + c + 1, :] * seen_land[c]
            for c in range(SDIM):
                total = total + kjac[r * SDIM + c:r * SDIM + c + 1, :] * seen_key[c]
            image.append(total * valid)
        sq_ref[...] += image[0] * image[0] + image[1] * image[1]
        if not with_scatter:
            return

        def scatter(acc_ref, jac, channels, hot, sel):
            placed = jnp.concatenate(
                [
                    (jac[c:c + 1, :] * image[0] + jac[channels + c:channels + c + 1, :] * image[1])
                    * sel
                    for c in range(channels)
                ],
                axis=0,
            )
            high, low = split_parts(placed)
            dims = (((1,), (1,)), ((), ()))
            acc_ref[...] += lax.dot_general(
                high, hot, dims, preferred_element_type=jnp.float32
            ) + lax.dot_general(low, hot, dims, preferred_element_type=jnp.float32)

        scatter(lacc_ref, ljac, 3, land_hot, land_sel)
        scatter(kacc_ref, kjac, SDIM, key_hot, key_sel)

    return kernel


def observe(valid, land_pos, key_pos, land_jac, key_jac, land_full, key_full, with_scatter):
    count = land_jac.shape[1]
    ltab = table_parts(land_full)
    ktab = table_parts(key_full)
    row = lambda i: (0, i)
    whole = lambda i: (0, 0)
    out_specs = [pl.BlockSpec((1, CHUNK), whole)]
    out_shape = [jax.ShapeDtypeStruct((1, CHUNK), jnp.float32)]
    if with_scatter:
        out_specs += [
            pl.BlockSpec((ltab.shape[0], LOW), whole),
            pl.BlockSpec((ktab.shape[0], LOW), whole),
        ]
        out_shape += [
            jax.ShapeDtypeStruct((ltab.shape[0], LOW), jnp.float32),
            jax.ShapeDtypeStruct((ktab.shape[0], LOW), jnp.float32),
        ]
    outs = pl.pallas_call(
        make_observe_kernel(with_scatter),
        grid=(count // CHUNK,),
        in_specs=[
            pl.BlockSpec((1, CHUNK), row),
            pl.BlockSpec((1, CHUNK), row),
            pl.BlockSpec((1, CHUNK), row),
            pl.BlockSpec((land_jac.shape[0], CHUNK), row),
            pl.BlockSpec((key_jac.shape[0], CHUNK), row),
            pl.BlockSpec(ltab.shape, whole),
            pl.BlockSpec(ktab.shape, whole),
        ],
        out_specs=out_specs,
        out_shape=out_shape,
        compiler_params=pltpu.CompilerParams(dimension_semantics=("arbitrary",)),
    )(valid, land_pos, key_pos, land_jac, key_jac, ltab, ktab)
    if not with_scatter:
        return jnp.sum(outs[0]), None, None
    sq, lacc, kacc = outs
    return jnp.sum(sq), lacc.reshape(land_full.shape), kacc.reshape(key_full.shape)


def shards(
    land_rhs,
    key_rhs,
    land_damp,
    key_damp,
    land_jac,
    key_jac,
    obs_landmark,
    obs_keyframe,
    live_blocks,
    preint,
):
    state_dev = key_rhs.shape[1]
    kf_count = lax.axis_size(KF)
    count = obs_landmark.shape[0]
    owner_block = obs_keyframe // state_dev
    key_pos = (owner_block // kf_count * state_dev + obs_keyframe % state_dev).reshape(1, count)
    land_dev = land_rhs.shape[1]
    me = lax.axis_index(KF)
    land_pos = (
        (me - obs_landmark // land_dev) % kf_count * land_dev + obs_landmark % land_dev
    ).reshape(1, count)
    live = live_blocks[0]
    valid = (jnp.arange(count, dtype=jnp.int32) // BLOCK < live).astype(jnp.float32).reshape(1, count)

    def reduce_all(values):
        return from_everyone(jnp.stack(values), LM_KF).sum(axis=0)

    def image_norms(dir_land, dir_key, with_scatter):
        land_full = shifted_gather(dir_land, KF)
        key_full = gather_directly(dir_key, LM, 1)
        squared, summed_land, summed_key = observe(
            valid, land_pos, key_pos, land_jac, key_jac, land_full, key_full, with_scatter
        )
        windowed = window_product(preint, dir_key)
        local_rr = jnp.sum(dir_land * dir_land) + jnp.sum(dir_key * dir_key)
        local_product = (
            squared
            + jnp.sum(land_damp * dir_land * dir_land)
            + jnp.sum(dir_key * (key_damp * dir_key + windowed))
        )
        if not with_scatter:
            rr, product = reduce_all([local_rr, local_product])
            return rr, product, None, None
        owned_land, partial = shifted_sum_with(
            summed_land, jnp.stack([local_rr, local_product]), KF
        )
        owned_key, total = sum_at_owner_with(summed_key, partial, LM)
        prod_land = owned_land + land_damp * dir_land
        prod_key = owned_key + key_damp * dir_key + windowed
        return total[0], total[1], prod_land, prod_key

    res_land, res_key = land_rhs, key_rhs
    norm_now, product, along_land, along_key = image_norms(res_land, res_key, True)
    step_size = norm_now / product
    sol_land = step_size * res_land
    sol_key = step_size * res_key
    dir_land, dir_key = res_land, res_key
    res_land = res_land - step_size * along_land
    res_key = res_key - step_size * along_key
    norm_next, product, _, _ = image_norms(res_land, res_key, False)
    beta_ratio = norm_next / norm_now
    step_size = norm_next / (product - beta_ratio * norm_next / step_size)
    dir_land = res_land + beta_ratio * dir_land
    dir_key = res_key + beta_ratio * dir_key
    sol_land = sol_land + step_size * dir_land
    sol_key = sol_key + step_size * dir_key
    return (sol_land, sol_key)


def solution(mesh):
    split = Mesh(mesh.devices.reshape(4, 4, 4, 2), ("lm_0", "lm_1", "kf_0", "kf_1"))
    in_specs = (
        P(None, LM_KF),
        P(None, LM_KF),
        P(None, LM_KF),
        P(None, LM_KF),
        P(None, LM_KF),
        P(None, LM_KF),
        P(LM_KF),
        P(LM_KF),
        P(LM_KF),
        P(None, LM_KF),
    )
    out_specs = (P(None, LM_KF), P(None, LM_KF))
    return jax.shard_map(
        shards, mesh=split, in_specs=in_specs, out_specs=out_specs, check_vma=False
    )
```

```python
import functools

import jax
import jax.numpy as jnp
from jax import lax
from jax.experimental import pallas as pl
from jax.experimental.pallas import tpu as pltpu
from jax.sharding import Mesh
from jax.sharding import PartitionSpec as P

WSTATES = 16
SDIM = 15
BLOCK = 128
ITERS = 2
WPAR = 240
LOW = 256
CHUNK = 2048
KF = ("kf_0", "kf_1")
LM = ("lm_0", "lm_1")
LM_KF = ("lm_0", "lm_1", "kf_0", "kf_1")


def window_product(preint, vectors):
    windows = preint.shape[1] // WPAR
    stacked = vectors.reshape(SDIM, windows, WSTATES).transpose(1, 2, 0).reshape(windows * WPAR)
    owner = jnp.arange(windows * WPAR, dtype=jnp.int32) // WPAR
    spread = jnp.where(
        owner[:, None] == jnp.arange(windows, dtype=jnp.int32)[None, :], stacked[:, None], 0.0
    )
    mapped = jnp.dot(preint, spread, precision=lax.Precision.HIGHEST)
    return (
        mapped.reshape(WSTATES, SDIM, windows).transpose(1, 2, 0).reshape(SDIM, windows * WSTATES)
    )


def split_parts(value):
    high = value.astype(jnp.bfloat16)
    low = (value - high.astype(jnp.float32)).astype(jnp.bfloat16)
    return high, low


def table_parts(full):
    channels, extent = full.shape
    folded = full.reshape(channels * (extent // LOW), LOW)
    high = lax.reduce_precision(folded, exponent_bits=8, mantissa_bits=7)
    return jnp.concatenate(
        [high.astype(jnp.bfloat16), (folded - high).astype(jnp.bfloat16)], axis=1
    )


def in_order(blocks, dim):
    shape = list(blocks.shape[1:])
    shape[dim] *= blocks.shape[0]
    return jnp.moveaxis(blocks, 0, dim).reshape(shape)


def from_everyone(value, axis):
    copies = jnp.broadcast_to(value, (lax.axis_size(axis), *value.shape))
    return lax.all_to_all(copies, axis, split_axis=0, concat_axis=0, tiled=True)


def gather_directly(value, axis, dim):
    return in_order(from_everyone(value, axis), dim)


def split_up(value, dim, devices):
    before, after = (value.shape[:dim], value.shape[dim + 1 :])
    return jnp.moveaxis(value.reshape(*before, devices, -1, *after), dim, 0)


def sum_at_owner(value, axis, dim):
    blocks = split_up(value, dim, lax.axis_size(axis))
    arrived = lax.all_to_all(blocks, axis, split_axis=0, concat_axis=0, tiled=True)
    return arrived.sum(axis=0)


def sum_at_owner_with(value, scalars, axis):
    devices = lax.axis_size(axis)
    blocks = split_up(value, 1, devices)
    extra = jnp.zeros((devices, 1, blocks.shape[2]), jnp.float32)
    extra = extra.at[:, 0, : scalars.shape[0]].set(scalars[None, :])
    blocks = jnp.concatenate([blocks, extra], axis=1)
    arrived = lax.all_to_all(blocks, axis, split_axis=0, concat_axis=0, tiled=True).sum(axis=0)
    return arrived[:-1], arrived[-1, : scalars.shape[0]]


def shifted_gather(value, axis):
    devices = lax.axis_size(axis)
    pieces = [value] + [
        lax.ppermute(value, axis, [(i, (i + k) % devices) for i in range(devices)])
        for k in range(1, devices)
    ]
    return jnp.concatenate(pieces, axis=1)


def shifted_sum_with(value, scalars, axis):
    devices = lax.axis_size(axis)
    width = value.shape[1] // devices
    extra = jnp.zeros((1, width), jnp.float32).at[0, : scalars.shape[0]].set(scalars)
    total = value[:, :width]
    arrived = [extra]
    for k in range(1, devices):
        block = jnp.concatenate([value[:, k * width:(k + 1) * width], extra], axis=0)
        moved = lax.ppermute(block, axis, [(i, (i - k) % devices) for i in range(devices)])
        total = total + moved[:-1]
        arrived.append(moved[-1:])
    me = lax.axis_index(axis)
    by_shift = jnp.concatenate(arrived, axis=0)[:, : scalars.shape[0]]
    by_source = jnp.take(by_shift, (jnp.arange(devices) - me) % devices, axis=0)
    return total, jnp.sum(by_source, axis=0)


def gather_with(value, scalars, axis):
    devices = lax.axis_size(axis)
    extra = jnp.zeros((1, value.shape[1]), jnp.float32).at[0, : scalars.shape[0]].set(scalars)
    block = jnp.concatenate([value, extra], axis=0)
    arrived = from_everyone(block, axis)
    total = jnp.sum(arrived[:, -1, : scalars.shape[0]], axis=0)
    return in_order(arrived[:, :-1], 1), total


def make_observe_kernel(with_scatter):
    def kernel(valid_ref, lpos_ref, kpos_ref, ljac_ref, kjac_ref, ltab_ref, ktab_ref, *outs):
        if with_scatter:
            sq_ref, lacc_ref, kacc_ref = outs
        else:
            (sq_ref,) = outs
        step = pl.program_id(0)

        @pl.when(step == 0)
        def _():
            for ref in outs:
                ref[...] = jnp.zeros_like(ref)

        span = valid_ref.shape[1]
        land_high = ltab_ref.shape[0] // 3
        key_high = ktab_ref.shape[0] // SDIM
        lpos = lpos_ref[...]
        kpos = kpos_ref[...]
        land_hot = (
            lax.broadcasted_iota(jnp.int32, (LOW, span), 0) == lpos % LOW
        ).astype(jnp.bfloat16)
        key_hot = (
            lax.broadcasted_iota(jnp.int32, (LOW, span), 0) == kpos % LOW
        ).astype(jnp.bfloat16)
        land_sel = (
            lax.broadcasted_iota(jnp.int32, (land_high, span), 0) == lpos // LOW
        ).astype(jnp.float32)
        key_sel = (
            lax.broadcasted_iota(jnp.int32, (key_high, span), 0) == kpos // LOW
        ).astype(jnp.float32)

        def gather(tab_ref, hot, sel, channels, high):
            rows = jnp.dot(
                tab_ref[...], jnp.concatenate([hot, hot], axis=0),
                preferred_element_type=jnp.float32,
            )
            return [
                jnp.sum(rows[c * high:(c + 1) * high, :] * sel, axis=0, keepdims=True)
                for c in range(channels)
            ]

        seen_land = gather(ltab_ref, land_hot, land_sel, 3, land_high)
        seen_key = gather(ktab_ref, key_hot, key_sel, SDIM, key_high)
        ljac = ljac_ref[...]
        kjac = kjac_ref[...]
        valid = valid_ref[...]
        image = []
        for r in range(2):
            total = ljac[r * 3:r * 3 + 1, :] * seen_land[0]
            for c in range(1, 3):
                total = total + ljac[r * 3 + c:r * 3 + c + 1, :] * seen_land[c]
            for c in range(SDIM):
                total = total + kjac[r * SDIM + c:r * SDIM + c + 1, :] * seen_key[c]
            image.append(total * valid)
        sq_ref[...] += image[0] * image[0] + image[1] * image[1]
        if not with_scatter:
            return

        def scatter(acc_ref, jac, channels, hot, sel):
            placed = jnp.concatenate(
                [
                    (jac[c:c + 1, :] * image[0] + jac[channels + c:channels + c + 1, :] * image[1])
                    * sel
                    for c in range(channels)
                ],
                axis=0,
            )
            high, low = split_parts(placed)
            dims = (((1,), (1,)), ((), ()))
            acc_ref[...] += lax.dot_general(
                high, hot, dims, preferred_element_type=jnp.float32
            ) + lax.dot_general(low, hot, dims, preferred_element_type=jnp.float32)

        scatter(lacc_ref, ljac, 3, land_hot, land_sel)
        scatter(kacc_ref, kjac, SDIM, key_hot, key_sel)

    return kernel


def observe(valid, land_pos, key_pos, land_jac, key_jac, land_full, key_full, with_scatter):
    count = land_jac.shape[1]
    ltab = table_parts(land_full)
    ktab = table_parts(key_full)
    row = lambda i: (0, i)
    whole = lambda i: (0, 0)
    out_specs = [pl.BlockSpec((1, CHUNK), whole)]
    out_shape = [jax.ShapeDtypeStruct((1, CHUNK), jnp.float32)]
    if with_scatter:
        out_specs += [
            pl.BlockSpec((ltab.shape[0], LOW), whole),
            pl.BlockSpec((ktab.shape[0], LOW), whole),
        ]
        out_shape += [
            jax.ShapeDtypeStruct((ltab.shape[0], LOW), jnp.float32),
            jax.ShapeDtypeStruct((ktab.shape[0], LOW), jnp.float32),
        ]
    outs = pl.pallas_call(
        make_observe_kernel(with_scatter),
        grid=(count // CHUNK,),
        in_specs=[
            pl.BlockSpec((1, CHUNK), row),
            pl.BlockSpec((1, CHUNK), row),
            pl.BlockSpec((1, CHUNK), row),
            pl.BlockSpec((land_jac.shape[0], CHUNK), row),
            pl.BlockSpec((key_jac.shape[0], CHUNK), row),
            pl.BlockSpec(ltab.shape, whole),
            pl.BlockSpec(ktab.shape, whole),
        ],
        out_specs=out_specs,
        out_shape=out_shape,
        compiler_params=pltpu.CompilerParams(dimension_semantics=("arbitrary",)),
    )(valid, land_pos, key_pos, land_jac, key_jac, ltab, ktab)
    if not with_scatter:
        return jnp.sum(outs[0]), None, None
    sq, lacc, kacc = outs
    return jnp.sum(sq), lacc.reshape(land_full.shape), kacc.reshape(key_full.shape)


def shards(
    land_rhs,
    key_rhs,
    land_damp,
    key_damp,
    land_jac,
    key_jac,
    obs_landmark,
    obs_keyframe,
    live_blocks,
    preint,
):
    state_dev = key_rhs.shape[1]
    kf_count = lax.axis_size(KF)
    count = obs_landmark.shape[0]
    owner_block = obs_keyframe // state_dev
    key_pos = (owner_block // kf_count * state_dev + obs_keyframe % state_dev).reshape(1, count)
    land_dev = land_rhs.shape[1]
    me = lax.axis_index(KF)
    land_pos = (
        (me - obs_landmark // land_dev) % kf_count * land_dev + obs_landmark % land_dev
    ).reshape(1, count)
    live = live_blocks[0]
    valid = (jnp.arange(count, dtype=jnp.int32) // BLOCK < live).astype(jnp.float32).reshape(1, count)

    def reduce_all(values):
        return from_everyone(jnp.stack(values), LM_KF).sum(axis=0)

    def local_terms(dir_land, dir_key, squared):
        windowed = window_product(preint, dir_key)
        local_rr = jnp.sum(dir_land * dir_land) + jnp.sum(dir_key * dir_key)
        local_product = (
            squared
            + jnp.sum(land_damp * dir_land * dir_land)
            + jnp.sum(dir_key * (key_damp * dir_key + windowed))
        )
        return windowed, jnp.stack([local_rr, local_product])

    first_land, first_key = land_rhs, key_rhs
    land_full = shifted_gather(first_land, KF)
    key_full = gather_directly(first_key, LM, 1)
    squared, summed_land, summed_key = observe(
        valid, land_pos, key_pos, land_jac, key_jac, land_full, key_full, True
    )
    windowed, scalars = local_terms(first_land, first_key, squared)
    owned_land, partial = shifted_sum_with(summed_land, scalars, KF)
    owned_key = sum_at_owner(summed_key, LM, 1)
    along_land = owned_land + land_damp * first_land
    along_key = owned_key + key_damp * first_key + windowed
    along_land_full = shifted_gather(along_land, KF)
    along_key_full, total = gather_with(along_key, partial, LM)
    norm_now, product = total[0], total[1]
    step_size = norm_now / product
    sol_land = step_size * first_land
    sol_key = step_size * first_key
    res_land = first_land - step_size * along_land
    res_key = first_key - step_size * along_key
    res_land_full = land_full - step_size * along_land_full
    res_key_full = key_full - step_size * along_key_full
    squared, _, _ = observe(
        valid, land_pos, key_pos, land_jac, key_jac, res_land_full, res_key_full, False
    )
    _, scalars = local_terms(res_land, res_key, squared)
    norm_next, product = reduce_all([scalars[0], scalars[1]])
    beta_ratio = norm_next / norm_now
    step_size = norm_next / (product - beta_ratio * norm_next / step_size)
    dir_land = res_land + beta_ratio * first_land
    dir_key = res_key + beta_ratio * first_key
    sol_land = sol_land + step_size * dir_land
    sol_key = sol_key + step_size * dir_key
    return (sol_land, sol_key)


def solution(mesh):
    split = Mesh(mesh.devices.reshape(4, 4, 4, 2), ("lm_0", "lm_1", "kf_0", "kf_1"))
    in_specs = (
        P(None, LM_KF),
        P(None, LM_KF),
        P(None, LM_KF),
        P(None, LM_KF),
        P(None, LM_KF),
        P(None, LM_KF),
        P(LM_KF),
        P(LM_KF),
        P(LM_KF),
        P(None, LM_KF),
    )
    out_specs = (P(None, LM_KF), P(None, LM_KF))
    return jax.shard_map(
        shards, mesh=split, in_specs=in_specs, out_specs=out_specs, check_vma=False
    )
```

```python
import functools

import jax
import jax.numpy as jnp
from jax import lax
from jax.experimental import pallas as pl
from jax.experimental.pallas import tpu as pltpu
from jax.sharding import Mesh
from jax.sharding import PartitionSpec as P

WSTATES = 16
SDIM = 15
BLOCK = 128
ITERS = 2
WPAR = 240
LOW = 256
CHUNK = 2048
KF = ("kf_0", "kf_1")
LM = ("lm_0", "lm_1")
LM_KF = ("lm_0", "lm_1", "kf_0", "kf_1")


def preint_parts(preint):
    high = lax.reduce_precision(preint, exponent_bits=8, mantissa_bits=7)
    high_part = high.astype(jnp.bfloat16)
    return jnp.concatenate([high_part, high_part, (preint - high).astype(jnp.bfloat16)], axis=1)


def window_product(parts, vectors):
    windows = parts.shape[1] // (3 * WPAR)
    stacked = vectors.reshape(SDIM, windows, WSTATES).transpose(1, 2, 0).reshape(windows * WPAR)
    owner = jnp.arange(windows * WPAR, dtype=jnp.int32) // WPAR
    spread = jnp.where(
        owner[:, None] == jnp.arange(windows, dtype=jnp.int32)[None, :], stacked[:, None], 0.0
    )
    spread_high = lax.reduce_precision(spread, exponent_bits=8, mantissa_bits=7)
    spread_parts = jnp.concatenate(
        [
            spread_high.astype(jnp.bfloat16),
            (spread - spread_high).astype(jnp.bfloat16),
            spread_high.astype(jnp.bfloat16),
        ],
        axis=0,
    )
    mapped = jnp.dot(parts, spread_parts, preferred_element_type=jnp.float32)
    return (
        mapped.reshape(WSTATES, SDIM, windows).transpose(1, 2, 0).reshape(SDIM, windows * WSTATES)
    )


def split_parts(value):
    high = value.astype(jnp.bfloat16)
    low = (value - high.astype(jnp.float32)).astype(jnp.bfloat16)
    return high, low


def table_parts(full):
    channels, extent = full.shape
    folded = full.reshape(channels * (extent // LOW), LOW)
    high = lax.reduce_precision(folded, exponent_bits=8, mantissa_bits=7)
    return jnp.concatenate(
        [high.astype(jnp.bfloat16), (folded - high).astype(jnp.bfloat16)], axis=1
    )


def in_order(blocks, dim):
    shape = list(blocks.shape[1:])
    shape[dim] *= blocks.shape[0]
    return jnp.moveaxis(blocks, 0, dim).reshape(shape)


def from_everyone(value, axis):
    copies = jnp.broadcast_to(value, (lax.axis_size(axis), *value.shape))
    return lax.all_to_all(copies, axis, split_axis=0, concat_axis=0, tiled=True)


def gather_directly(value, axis, dim):
    return in_order(from_everyone(value, axis), dim)


def split_up(value, dim, devices):
    before, after = (value.shape[:dim], value.shape[dim + 1 :])
    return jnp.moveaxis(value.reshape(*before, devices, -1, *after), dim, 0)


def sum_at_owner(value, axis, dim):
    blocks = split_up(value, dim, lax.axis_size(axis))
    arrived = lax.all_to_all(blocks, axis, split_axis=0, concat_axis=0, tiled=True)
    return arrived.sum(axis=0)


def sum_at_owner_with(value, scalars, axis):
    devices = lax.axis_size(axis)
    blocks = split_up(value, 1, devices)
    extra = jnp.zeros((devices, 1, blocks.shape[2]), jnp.float32)
    extra = extra.at[:, 0, : scalars.shape[0]].set(scalars[None, :])
    blocks = jnp.concatenate([blocks, extra], axis=1)
    arrived = lax.all_to_all(blocks, axis, split_axis=0, concat_axis=0, tiled=True).sum(axis=0)
    return arrived[:-1], arrived[-1, : scalars.shape[0]]


def shifted_gather(value, axis):
    devices = lax.axis_size(axis)
    pieces = [value] + [
        lax.ppermute(value, axis, [(i, (i + k) % devices) for i in range(devices)])
        for k in range(1, devices)
    ]
    return jnp.concatenate(pieces, axis=1)


def shifted_sum_with(value, scalars, axis):
    devices = lax.axis_size(axis)
    width = value.shape[1] // devices
    extra = jnp.zeros((1, width), jnp.float32).at[0, : scalars.shape[0]].set(scalars)
    total = value[:, :width]
    arrived = [extra]
    for k in range(1, devices):
        block = jnp.concatenate([value[:, k * width:(k + 1) * width], extra], axis=0)
        moved = lax.ppermute(block, axis, [(i, (i - k) % devices) for i in range(devices)])
        total = total + moved[:-1]
        arrived.append(moved[-1:])
    me = lax.axis_index(axis)
    by_shift = jnp.concatenate(arrived, axis=0)[:, : scalars.shape[0]]
    by_source = jnp.take(by_shift, (jnp.arange(devices) - me) % devices, axis=0)
    return total, jnp.sum(by_source, axis=0)


def gather_with(value, scalars, axis):
    devices = lax.axis_size(axis)
    extra = jnp.zeros((1, value.shape[1]), jnp.float32).at[0, : scalars.shape[0]].set(scalars)
    block = jnp.concatenate([value, extra], axis=0)
    arrived = from_everyone(block, axis)
    total = jnp.sum(arrived[:, -1, : scalars.shape[0]], axis=0)
    return in_order(arrived[:, :-1], 1), total


def make_observe_kernel(with_scatter):
    def kernel(valid_ref, lpos_ref, kpos_ref, ljac_ref, kjac_ref, ltab_ref, ktab_ref, *outs):
        if with_scatter:
            sq_ref, lacc_ref, kacc_ref = outs
        else:
            (sq_ref,) = outs
        step = pl.program_id(0)

        @pl.when(step == 0)
        def _():
            for ref in outs:
                ref[...] = jnp.zeros_like(ref)

        span = valid_ref.shape[1]
        land_high = ltab_ref.shape[0] // 3
        key_high = ktab_ref.shape[0] // SDIM
        lpos = lpos_ref[...]
        kpos = kpos_ref[...]
        land_hot = (
            lax.broadcasted_iota(jnp.int32, (LOW, span), 0) == lpos % LOW
        ).astype(jnp.bfloat16)
        key_hot = (
            lax.broadcasted_iota(jnp.int32, (LOW, span), 0) == kpos % LOW
        ).astype(jnp.bfloat16)
        land_sel = (
            lax.broadcasted_iota(jnp.int32, (land_high, span), 0) == lpos // LOW
        ).astype(jnp.float32)
        key_sel = (
            lax.broadcasted_iota(jnp.int32, (key_high, span), 0) == kpos // LOW
        ).astype(jnp.float32)

        def gather(tab_ref, hot, sel, channels, high):
            rows = jnp.dot(
                tab_ref[...], jnp.concatenate([hot, hot], axis=0),
                preferred_element_type=jnp.float32,
            )
            return [
                jnp.sum(rows[c * high:(c + 1) * high, :] * sel, axis=0, keepdims=True)
                for c in range(channels)
            ]

        seen_land = gather(ltab_ref, land_hot, land_sel, 3, land_high)
        seen_key = gather(ktab_ref, key_hot, key_sel, SDIM, key_high)
        ljac = ljac_ref[...]
        kjac = kjac_ref[...]
        valid = valid_ref[...]
        image = []
        for r in range(2):
            total = ljac[r * 3:r * 3 + 1, :] * seen_land[0]
            for c in range(1, 3):
                total = total + ljac[r * 3 + c:r * 3 + c + 1, :] * seen_land[c]
            for c in range(SDIM):
                total = total + kjac[r * SDIM + c:r * SDIM + c + 1, :] * seen_key[c]
            image.append(total * valid)
        sq_ref[...] += image[0] * image[0] + image[1] * image[1]
        if not with_scatter:
            return

        def scatter(acc_ref, jac, channels, hot, sel):
            placed = jnp.concatenate(
                [
                    (jac[c:c + 1, :] * image[0] + jac[channels + c:channels + c + 1, :] * image[1])
                    * sel
                    for c in range(channels)
                ],
                axis=0,
            )
            high, low = split_parts(placed)
            dims = (((1,), (1,)), ((), ()))
            acc_ref[...] += lax.dot_general(
                high, hot, dims, preferred_element_type=jnp.float32
            ) + lax.dot_general(low, hot, dims, preferred_element_type=jnp.float32)

        scatter(lacc_ref, ljac, 3, land_hot, land_sel)
        scatter(kacc_ref, kjac, SDIM, key_hot, key_sel)

    return kernel


def observe(valid, land_pos, key_pos, land_jac, key_jac, land_full, key_full, with_scatter):
    count = land_jac.shape[1]
    ltab = table_parts(land_full)
    ktab = table_parts(key_full)
    row = lambda i: (0, i)
    whole = lambda i: (0, 0)
    out_specs = [pl.BlockSpec((1, CHUNK), whole)]
    out_shape = [jax.ShapeDtypeStruct((1, CHUNK), jnp.float32)]
    if with_scatter:
        out_specs += [
            pl.BlockSpec((ltab.shape[0], LOW), whole),
            pl.BlockSpec((ktab.shape[0], LOW), whole),
        ]
        out_shape += [
            jax.ShapeDtypeStruct((ltab.shape[0], LOW), jnp.float32),
            jax.ShapeDtypeStruct((ktab.shape[0], LOW), jnp.float32),
        ]
    outs = pl.pallas_call(
        make_observe_kernel(with_scatter),
        grid=(count // CHUNK,),
        in_specs=[
            pl.BlockSpec((1, CHUNK), row),
            pl.BlockSpec((1, CHUNK), row),
            pl.BlockSpec((1, CHUNK), row),
            pl.BlockSpec((land_jac.shape[0], CHUNK), row),
            pl.BlockSpec((key_jac.shape[0], CHUNK), row),
            pl.BlockSpec(ltab.shape, whole),
            pl.BlockSpec(ktab.shape, whole),
        ],
        out_specs=out_specs,
        out_shape=out_shape,
        compiler_params=pltpu.CompilerParams(dimension_semantics=("arbitrary",)),
    )(valid, land_pos, key_pos, land_jac, key_jac, ltab, ktab)
    if not with_scatter:
        return jnp.sum(outs[0]), None, None
    sq, lacc, kacc = outs
    return jnp.sum(sq), lacc.reshape(land_full.shape), kacc.reshape(key_full.shape)


def shards(
    land_rhs,
    key_rhs,
    land_damp,
    key_damp,
    land_jac,
    key_jac,
    obs_landmark,
    obs_keyframe,
    live_blocks,
    preint,
):
    state_dev = key_rhs.shape[1]
    kf_count = lax.axis_size(KF)
    count = obs_landmark.shape[0]
    owner_block = obs_keyframe // state_dev
    key_pos = (owner_block // kf_count * state_dev + obs_keyframe % state_dev).reshape(1, count)
    land_dev = land_rhs.shape[1]
    me = lax.axis_index(KF)
    land_pos = (
        (me - obs_landmark // land_dev) % kf_count * land_dev + obs_landmark % land_dev
    ).reshape(1, count)
    live = live_blocks[0]
    valid = (jnp.arange(count, dtype=jnp.int32) // BLOCK < live).astype(jnp.float32).reshape(1, count)

    def reduce_all(values):
        return from_everyone(jnp.stack(values), LM_KF).sum(axis=0)

    preint_split = preint_parts(preint)

    def local_terms(dir_land, dir_key, squared):
        windowed = window_product(preint_split, dir_key)
        local_rr = jnp.sum(dir_land * dir_land) + jnp.sum(dir_key * dir_key)
        local_product = (
            squared
            + jnp.sum(land_damp * dir_land * dir_land)
            + jnp.sum(dir_key * (key_damp * dir_key + windowed))
        )
        return windowed, jnp.stack([local_rr, local_product])

    first_land, first_key = land_rhs, key_rhs
    land_full = shifted_gather(first_land, KF)
    key_full = gather_directly(first_key, LM, 1)
    squared, summed_land, summed_key = observe(
        valid, land_pos, key_pos, land_jac, key_jac, land_full, key_full, True
    )
    windowed, scalars = local_terms(first_land, first_key, squared)
    owned_land, partial = shifted_sum_with(summed_land, scalars, KF)
    owned_key = sum_at_owner(summed_key, LM, 1)
    along_land = owned_land + land_damp * first_land
    along_key = owned_key + key_damp * first_key + windowed
    along_land_full = shifted_gather(along_land, KF)
    along_key_full, total = gather_with(along_key, partial, LM)
    norm_now, product = total[0], total[1]
    step_size = norm_now / product
    sol_land = step_size * first_land
    sol_key = step_size * first_key
    res_land = first_land - step_size * along_land
    res_key = first_key - step_size * along_key
    res_land_full = land_full - step_size * along_land_full
    res_key_full = key_full - step_size * along_key_full
    squared, _, _ = observe(
        valid, land_pos, key_pos, land_jac, key_jac, res_land_full, res_key_full, False
    )
    _, scalars = local_terms(res_land, res_key, squared)
    norm_next, product = reduce_all([scalars[0], scalars[1]])
    beta_ratio = norm_next / norm_now
    step_size = norm_next / (product - beta_ratio * norm_next / step_size)
    dir_land = res_land + beta_ratio * first_land
    dir_key = res_key + beta_ratio * first_key
    sol_land = sol_land + step_size * dir_land
    sol_key = sol_key + step_size * dir_key
    return (sol_land, sol_key)


def solution(mesh):
    split = Mesh(mesh.devices.reshape(4, 4, 4, 2), ("lm_0", "lm_1", "kf_0", "kf_1"))
    in_specs = (
        P(None, LM_KF),
        P(None, LM_KF),
        P(None, LM_KF),
        P(None, LM_KF),
        P(None, LM_KF),
        P(None, LM_KF),
        P(LM_KF),
        P(LM_KF),
        P(LM_KF),
        P(None, LM_KF),
    )
    out_specs = (P(None, LM_KF), P(None, LM_KF))
    return jax.shard_map(
        shards, mesh=split, in_specs=in_specs, out_specs=out_specs, check_vma=False
    )
```

```python
import functools

import jax
import jax.numpy as jnp
from jax import lax
from jax.experimental import pallas as pl
from jax.experimental.pallas import tpu as pltpu
from jax.sharding import Mesh
from jax.sharding import PartitionSpec as P

WSTATES = 16
SDIM = 15
BLOCK = 128
ITERS = 2
WPAR = 240
LOW = 256
CHUNK = 2048
KF = ("kf_0", "kf_1")
LM = ("lm_0", "lm_1")
LM_KF = ("lm_0", "lm_1", "kf_0", "kf_1")


def window_product(preint, vectors):
    windows = preint.shape[1] // WPAR
    stacked = vectors.reshape(SDIM, windows, WSTATES).transpose(1, 2, 0).reshape(windows * WPAR)
    owner = jnp.arange(windows * WPAR, dtype=jnp.int32) // WPAR
    spread = jnp.where(
        owner[:, None] == jnp.arange(windows, dtype=jnp.int32)[None, :], stacked[:, None], 0.0
    )
    mapped = jnp.dot(preint, spread, precision=lax.Precision.HIGHEST)
    return (
        mapped.reshape(WSTATES, SDIM, windows).transpose(1, 2, 0).reshape(SDIM, windows * WSTATES)
    )


def split_parts(value):
    high = value.astype(jnp.bfloat16)
    low = (value - high.astype(jnp.float32)).astype(jnp.bfloat16)
    return high, low


def table_parts(full):
    channels, extent = full.shape
    folded = full.reshape(channels * (extent // LOW), LOW)
    high = lax.reduce_precision(folded, exponent_bits=8, mantissa_bits=7)
    return jnp.concatenate(
        [high.astype(jnp.bfloat16), (folded - high).astype(jnp.bfloat16)], axis=1
    )


def in_order(blocks, dim):
    shape = list(blocks.shape[1:])
    shape[dim] *= blocks.shape[0]
    return jnp.moveaxis(blocks, 0, dim).reshape(shape)


def from_everyone(value, axis):
    copies = jnp.broadcast_to(value, (lax.axis_size(axis), *value.shape))
    return lax.all_to_all(copies, axis, split_axis=0, concat_axis=0, tiled=True)


def gather_directly(value, axis, dim):
    return in_order(from_everyone(value, axis), dim)


def split_up(value, dim, devices):
    before, after = (value.shape[:dim], value.shape[dim + 1 :])
    return jnp.moveaxis(value.reshape(*before, devices, -1, *after), dim, 0)


def sum_at_owner(value, axis, dim):
    blocks = split_up(value, dim, lax.axis_size(axis))
    arrived = lax.all_to_all(blocks, axis, split_axis=0, concat_axis=0, tiled=True)
    return arrived.sum(axis=0)


def sum_at_owner_with(value, scalars, axis):
    devices = lax.axis_size(axis)
    blocks = split_up(value, 1, devices)
    extra = jnp.zeros((devices, 1, blocks.shape[2]), jnp.float32)
    extra = extra.at[:, 0, : scalars.shape[0]].set(scalars[None, :])
    blocks = jnp.concatenate([blocks, extra], axis=1)
    arrived = lax.all_to_all(blocks, axis, split_axis=0, concat_axis=0, tiled=True).sum(axis=0)
    return arrived[:-1], arrived[-1, : scalars.shape[0]]


def make_observe_kernel(with_scatter):
    def kernel(valid_ref, lpos_ref, kpos_ref, ljac_ref, kjac_ref, ltab_ref, ktab_ref, *outs):
        if with_scatter:
            sq_ref, lacc_ref, kacc_ref = outs
        else:
            (sq_ref,) = outs
        step = pl.program_id(0)

        @pl.when(step == 0)
        def _():
            for ref in outs:
                ref[...] = jnp.zeros_like(ref)

        span = valid_ref.shape[1]
        land_high = ltab_ref.shape[0] // 3
        key_high = ktab_ref.shape[0] // SDIM
        lpos = lpos_ref[...]
        kpos = kpos_ref[...]
        land_hot = (
            lax.broadcasted_iota(jnp.int32, (LOW, span), 0) == lpos % LOW
        ).astype(jnp.bfloat16)
        key_hot = (
            lax.broadcasted_iota(jnp.int32, (LOW, span), 0) == kpos % LOW
        ).astype(jnp.bfloat16)
        land_sel = (
            lax.broadcasted_iota(jnp.int32, (land_high, span), 0) == lpos // LOW
        ).astype(jnp.float32)
        key_sel = (
            lax.broadcasted_iota(jnp.int32, (key_high, span), 0) == kpos // LOW
        ).astype(jnp.float32)

        def gather(tab_ref, hot, sel, channels, high):
            rows = jnp.dot(
                tab_ref[...], jnp.concatenate([hot, hot], axis=0),
                preferred_element_type=jnp.float32,
            )
            return [
                jnp.sum(rows[c * high:(c + 1) * high, :] * sel, axis=0, keepdims=True)
                for c in range(channels)
            ]

        seen_land = gather(ltab_ref, land_hot, land_sel, 3, land_high)
        seen_key = gather(ktab_ref, key_hot, key_sel, SDIM, key_high)
        ljac = ljac_ref[...]
        kjac = kjac_ref[...]
        valid = valid_ref[...]
        image = []
        for r in range(2):
            total = ljac[r * 3:r * 3 + 1, :] * seen_land[0]
            for c in range(1, 3):
                total = total + ljac[r * 3 + c:r * 3 + c + 1, :] * seen_land[c]
            for c in range(SDIM):
                total = total + kjac[r * SDIM + c:r * SDIM + c + 1, :] * seen_key[c]
            image.append(total * valid)
        sq_ref[...] += image[0] * image[0] + image[1] * image[1]
        if not with_scatter:
            return

        def scatter(acc_ref, jac, channels, hot, sel):
            mask = sel.astype(jnp.bfloat16)
            high_rows, low_rows = [], []
            for c in range(channels):
                back = jac[c:c + 1, :] * image[0] + jac[channels + c:channels + c + 1, :] * image[1]
                back_high, back_low = split_parts(back)
                high_rows.append(back_high * mask)
                low_rows.append(back_low * mask)
            high = jnp.concatenate(high_rows, axis=0)
            low = jnp.concatenate(low_rows, axis=0)
            dims = (((1,), (1,)), ((), ()))
            acc_ref[...] += lax.dot_general(
                high, hot, dims, preferred_element_type=jnp.float32
            ) + lax.dot_general(low, hot, dims, preferred_element_type=jnp.float32)

        scatter(lacc_ref, ljac, 3, land_hot, land_sel)
        scatter(kacc_ref, kjac, SDIM, key_hot, key_sel)

    return kernel


def observe(valid, land_pos, key_pos, land_jac, key_jac, land_full, key_full, with_scatter):
    count = land_jac.shape[1]
    ltab = table_parts(land_full)
    ktab = table_parts(key_full)
    row = lambda i: (0, i)
    whole = lambda i: (0, 0)
    out_specs = [pl.BlockSpec((1, CHUNK), whole)]
    out_shape = [jax.ShapeDtypeStruct((1, CHUNK), jnp.float32)]
    if with_scatter:
        out_specs += [
            pl.BlockSpec((ltab.shape[0], LOW), whole),
            pl.BlockSpec((ktab.shape[0], LOW), whole),
        ]
        out_shape += [
            jax.ShapeDtypeStruct((ltab.shape[0], LOW), jnp.float32),
            jax.ShapeDtypeStruct((ktab.shape[0], LOW), jnp.float32),
        ]
    outs = pl.pallas_call(
        make_observe_kernel(with_scatter),
        grid=(count // CHUNK,),
        in_specs=[
            pl.BlockSpec((1, CHUNK), row),
            pl.BlockSpec((1, CHUNK), row),
            pl.BlockSpec((1, CHUNK), row),
            pl.BlockSpec((land_jac.shape[0], CHUNK), row),
            pl.BlockSpec((key_jac.shape[0], CHUNK), row),
            pl.BlockSpec(ltab.shape, whole),
            pl.BlockSpec(ktab.shape, whole),
        ],
        out_specs=out_specs,
        out_shape=out_shape,
        compiler_params=pltpu.CompilerParams(dimension_semantics=("arbitrary",)),
    )(valid, land_pos, key_pos, land_jac, key_jac, ltab, ktab)
    if not with_scatter:
        return jnp.sum(outs[0]), None, None
    sq, lacc, kacc = outs
    return jnp.sum(sq), lacc.reshape(land_full.shape), kacc.reshape(key_full.shape)


def shards(
    land_rhs,
    key_rhs,
    land_damp,
    key_damp,
    land_jac,
    key_jac,
    obs_landmark,
    obs_keyframe,
    live_blocks,
    preint,
):
    state_dev = key_rhs.shape[1]
    kf_count = lax.axis_size(KF)
    count = obs_landmark.shape[0]
    owner_block = obs_keyframe // state_dev
    key_pos = (owner_block // kf_count * state_dev + obs_keyframe % state_dev).reshape(1, count)
    land_pos = obs_landmark.reshape(1, count)
    live = live_blocks[0]
    valid = (jnp.arange(count, dtype=jnp.int32) // BLOCK < live).astype(jnp.float32).reshape(1, count)

    def reduce_all(values):
        return from_everyone(jnp.stack(values), LM_KF).sum(axis=0)

    def image_norms(dir_land, dir_key, with_scatter):
        land_full = gather_directly(dir_land, KF, 1)
        key_full = gather_directly(dir_key, LM, 1)
        squared, summed_land, summed_key = observe(
            valid, land_pos, key_pos, land_jac, key_jac, land_full, key_full, with_scatter
        )
        windowed = window_product(preint, dir_key)
        local_rr = jnp.sum(dir_land * dir_land) + jnp.sum(dir_key * dir_key)
        local_product = (
            squared
            + jnp.sum(land_damp * dir_land * dir_land)
            + jnp.sum(dir_key * (key_damp * dir_key + windowed))
        )
        if not with_scatter:
            rr, product = reduce_all([local_rr, local_product])
            return rr, product, None, None
        owned_land, partial = sum_at_owner_with(
            summed_land, jnp.stack([local_rr, local_product]), KF
        )
        owned_key, total = sum_at_owner_with(summed_key, partial, LM)
        prod_land = owned_land + land_damp * dir_land
        prod_key = owned_key + key_damp * dir_key + windowed
        return total[0], total[1], prod_land, prod_key

    res_land, res_key = land_rhs, key_rhs
    norm_now, product, along_land, along_key = image_norms(res_land, res_key, True)
    step_size = norm_now / product
    sol_land = step_size * res_land
    sol_key = step_size * res_key
    dir_land, dir_key = res_land, res_key
    res_land = res_land - step_size * along_land
    res_key = res_key - step_size * along_key
    norm_next, product, _, _ = image_norms(res_land, res_key, False)
    beta_ratio = norm_next / norm_now
    step_size = norm_next / (product - beta_ratio * norm_next / step_size)
    dir_land = res_land + beta_ratio * dir_land
    dir_key = res_key + beta_ratio * dir_key
    sol_land = sol_land + step_size * dir_land
    sol_key = sol_key + step_size * dir_key
    return (sol_land, sol_key)


def solution(mesh):
    split = Mesh(mesh.devices.reshape(4, 4, 4, 2), ("lm_0", "lm_1", "kf_0", "kf_1"))
    in_specs = (
        P(None, LM_KF),
        P(None, LM_KF),
        P(None, LM_KF),
        P(None, LM_KF),
        P(None, LM_KF),
        P(None, LM_KF),
        P(LM_KF),
        P(LM_KF),
        P(LM_KF),
        P(None, LM_KF),
    )
    out_specs = (P(None, LM_KF), P(None, LM_KF))
    return jax.shard_map(
        shards, mesh=split, in_specs=in_specs, out_specs=out_specs, check_vma=False
    )
```

```python
import functools

import jax
import jax.numpy as jnp
from jax import lax
from jax.experimental import pallas as pl
from jax.experimental.pallas import tpu as pltpu
from jax.sharding import Mesh
from jax.sharding import PartitionSpec as P

WSTATES = 16
SDIM = 15
BLOCK = 128
ITERS = 2
WPAR = 240
LOW = 256
CHUNK = 2048
KF = ("kf_0", "kf_1")
LM = ("lm_0", "lm_1")
LM_KF = ("lm_0", "lm_1", "kf_0", "kf_1")


def window_product(preint, vectors):
    windows = preint.shape[1] // WPAR
    stacked = vectors.reshape(SDIM, windows, WSTATES).transpose(1, 2, 0).reshape(windows * WPAR)
    owner = jnp.arange(windows * WPAR, dtype=jnp.int32) // WPAR
    spread = jnp.where(
        owner[:, None] == jnp.arange(windows, dtype=jnp.int32)[None, :], stacked[:, None], 0.0
    )
    mapped = jnp.dot(preint, spread, precision=lax.Precision.HIGHEST)
    return (
        mapped.reshape(WSTATES, SDIM, windows).transpose(1, 2, 0).reshape(SDIM, windows * WSTATES)
    )


def split_parts(value):
    high = value.astype(jnp.bfloat16)
    low = (value - high.astype(jnp.float32)).astype(jnp.bfloat16)
    return high, low


def table_parts(full):
    channels, extent = full.shape
    folded = full.reshape(channels * (extent // LOW), LOW)
    high = lax.reduce_precision(folded, exponent_bits=8, mantissa_bits=7)
    return jnp.concatenate(
        [high.astype(jnp.bfloat16), (folded - high).astype(jnp.bfloat16)], axis=1
    )


def in_order(blocks, dim):
    shape = list(blocks.shape[1:])
    shape[dim] *= blocks.shape[0]
    return jnp.moveaxis(blocks, 0, dim).reshape(shape)


def from_everyone(value, axis):
    copies = jnp.broadcast_to(value, (lax.axis_size(axis), *value.shape))
    return lax.all_to_all(copies, axis, split_axis=0, concat_axis=0, tiled=True)


def gather_directly(value, axis, dim):
    return in_order(from_everyone(value, axis), dim)


def split_up(value, dim, devices):
    before, after = (value.shape[:dim], value.shape[dim + 1 :])
    return jnp.moveaxis(value.reshape(*before, devices, -1, *after), dim, 0)


def sum_at_owner(value, axis, dim):
    blocks = split_up(value, dim, lax.axis_size(axis))
    arrived = lax.all_to_all(blocks, axis, split_axis=0, concat_axis=0, tiled=True)
    return arrived.sum(axis=0)


def sum_at_owner_with(value, scalars, axis):
    devices = lax.axis_size(axis)
    blocks = split_up(value, 1, devices)
    extra = jnp.zeros((devices, 1, blocks.shape[2]), jnp.float32)
    extra = extra.at[:, 0, : scalars.shape[0]].set(scalars[None, :])
    blocks = jnp.concatenate([blocks, extra], axis=1)
    arrived = lax.all_to_all(blocks, axis, split_axis=0, concat_axis=0, tiled=True).sum(axis=0)
    return arrived[:-1], arrived[-1, : scalars.shape[0]]


def make_observe_kernel(with_scatter):
    def kernel(valid_ref, lpos_ref, kpos_ref, ljac_ref, kjac_ref, ltab_ref, ktab_ref, *outs):
        if with_scatter:
            sq_ref, lacc_ref, kacc_ref = outs
        else:
            (sq_ref,) = outs
        step = pl.program_id(0)

        @pl.when(step == 0)
        def _():
            for ref in outs:
                ref[...] = jnp.zeros_like(ref)

        span = valid_ref.shape[1]
        land_high = ltab_ref.shape[0] // 3
        key_high = ktab_ref.shape[0] // SDIM
        lpos = lpos_ref[...]
        kpos = kpos_ref[...]
        land_hot = (
            lax.broadcasted_iota(jnp.int32, (LOW, span), 0) == lpos % LOW
        ).astype(jnp.bfloat16)
        key_hot = (
            lax.broadcasted_iota(jnp.int32, (LOW, span), 0) == kpos % LOW
        ).astype(jnp.bfloat16)
        land_sel = (
            lax.broadcasted_iota(jnp.int32, (land_high, span), 0) == lpos // LOW
        ).astype(jnp.float32)
        key_sel = (
            lax.broadcasted_iota(jnp.int32, (key_high, span), 0) == kpos // LOW
        ).astype(jnp.float32)

        def gather(tab_ref, hot, sel, channels, high):
            rows = jnp.dot(
                tab_ref[...], jnp.concatenate([hot, hot], axis=0),
                preferred_element_type=jnp.float32,
            )
            return [
                jnp.sum(rows[c * high:(c + 1) * high, :] * sel, axis=0, keepdims=True)
                for c in range(channels)
            ]

        seen_land = gather(ltab_ref, land_hot, land_sel, 3, land_high)
        seen_key = gather(ktab_ref, key_hot, key_sel, SDIM, key_high)
        ljac = ljac_ref[...]
        kjac = kjac_ref[...]
        valid = valid_ref[...]
        image = []
        for r in range(2):
            total = ljac[r * 3:r * 3 + 1, :] * seen_land[0]
            for c in range(1, 3):
                total = total + ljac[r * 3 + c:r * 3 + c + 1, :] * seen_land[c]
            for c in range(SDIM):
                total = total + kjac[r * SDIM + c:r * SDIM + c + 1, :] * seen_key[c]
            image.append(total * valid)
        sq_ref[...] += image[0] * image[0] + image[1] * image[1]
        if not with_scatter:
            return

        def scatter(acc_ref, jac, channels, hot, sel):
            mask = sel.astype(jnp.bfloat16)
            high_rows, low_rows = [], []
            for c in range(channels):
                back = jac[c:c + 1, :] * image[0] + jac[channels + c:channels + c + 1, :] * image[1]
                back_high, back_low = split_parts(back)
                high_rows.append(back_high * mask)
                low_rows.append(back_low * mask)
            high = jnp.concatenate(high_rows, axis=0)
            low = jnp.concatenate(low_rows, axis=0)
            dims = (((1,), (1,)), ((), ()))
            acc_ref[...] += lax.dot_general(
                high, hot, dims, preferred_element_type=jnp.float32
            ) + lax.dot_general(low, hot, dims, preferred_element_type=jnp.float32)

        scatter(lacc_ref, ljac, 3, land_hot, land_sel)
        scatter(kacc_ref, kjac, SDIM, key_hot, key_sel)

    return kernel


def observe(valid, land_pos, key_pos, land_jac, key_jac, land_full, key_full, with_scatter):
    count = land_jac.shape[1]
    ltab = table_parts(land_full)
    ktab = table_parts(key_full)
    row = lambda i: (0, i)
    whole = lambda i: (0, 0)
    out_specs = [pl.BlockSpec((1, CHUNK), whole)]
    out_shape = [jax.ShapeDtypeStruct((1, CHUNK), jnp.float32)]
    if with_scatter:
        out_specs += [
            pl.BlockSpec((ltab.shape[0], LOW), whole),
            pl.BlockSpec((ktab.shape[0], LOW), whole),
        ]
        out_shape += [
            jax.ShapeDtypeStruct((ltab.shape[0], LOW), jnp.float32),
            jax.ShapeDtypeStruct((ktab.shape[0], LOW), jnp.float32),
        ]
    outs = pl.pallas_call(
        make_observe_kernel(with_scatter),
        grid=(count // CHUNK,),
        in_specs=[
            pl.BlockSpec((1, CHUNK), row),
            pl.BlockSpec((1, CHUNK), row),
            pl.BlockSpec((1, CHUNK), row),
            pl.BlockSpec((land_jac.shape[0], CHUNK), row),
            pl.BlockSpec((key_jac.shape[0], CHUNK), row),
            pl.BlockSpec(ltab.shape, whole),
            pl.BlockSpec(ktab.shape, whole),
        ],
        out_specs=out_specs,
        out_shape=out_shape,
        compiler_params=pltpu.CompilerParams(dimension_semantics=("arbitrary",)),
    )(valid, land_pos, key_pos, land_jac, key_jac, ltab, ktab)
    if not with_scatter:
        return jnp.sum(outs[0]), None, None
    sq, lacc, kacc = outs
    return jnp.sum(sq), lacc.reshape(land_full.shape), kacc.reshape(key_full.shape)


def shards(
    land_rhs,
    key_rhs,
    land_damp,
    key_damp,
    land_jac,
    key_jac,
    obs_landmark,
    obs_keyframe,
    live_blocks,
    preint,
):
    state_dev = key_rhs.shape[1]
    kf_count = lax.axis_size(KF)
    count = obs_landmark.shape[0]
    owner_block = obs_keyframe // state_dev
    key_pos = (owner_block // kf_count * state_dev + obs_keyframe % state_dev).reshape(1, count)
    land_pos = obs_landmark.reshape(1, count)
    live = live_blocks[0]
    valid = (jnp.arange(count, dtype=jnp.int32) // BLOCK < live).astype(jnp.float32).reshape(1, count)

    def reduce_all(values):
        return from_everyone(jnp.stack(values), LM_KF).sum(axis=0)

    def image_norms(dir_land, dir_key, with_scatter):
        key_full = gather_directly(dir_key, LM, 1)
        after_key, key_full = lax.optimization_barrier((dir_land, key_full))
        land_full = gather_directly(after_key, KF, 1)
        squared, summed_land, summed_key = observe(
            valid, land_pos, key_pos, land_jac, key_jac, land_full, key_full, with_scatter
        )
        windowed = window_product(preint, dir_key)
        local_rr = jnp.sum(dir_land * dir_land) + jnp.sum(dir_key * dir_key)
        local_product = (
            squared
            + jnp.sum(land_damp * dir_land * dir_land)
            + jnp.sum(dir_key * (key_damp * dir_key + windowed))
        )
        if not with_scatter:
            rr, product = reduce_all([local_rr, local_product])
            return rr, product, None, None
        owned_land, partial = sum_at_owner_with(
            summed_land, jnp.stack([local_rr, local_product]), KF
        )
        owned_key, total = sum_at_owner_with(summed_key, partial, LM)
        prod_land = owned_land + land_damp * dir_land
        prod_key = owned_key + key_damp * dir_key + windowed
        return total[0], total[1], prod_land, prod_key

    res_land, res_key = land_rhs, key_rhs
    norm_now, product, along_land, along_key = image_norms(res_land, res_key, True)
    step_size = norm_now / product
    sol_land = step_size * res_land
    sol_key = step_size * res_key
    dir_land, dir_key = res_land, res_key
    res_land = res_land - step_size * along_land
    res_key = res_key - step_size * along_key
    norm_next, product, _, _ = image_norms(res_land, res_key, False)
    beta_ratio = norm_next / norm_now
    step_size = norm_next / (product - beta_ratio * norm_next / step_size)
    dir_land = res_land + beta_ratio * dir_land
    dir_key = res_key + beta_ratio * dir_key
    sol_land = sol_land + step_size * dir_land
    sol_key = sol_key + step_size * dir_key
    return (sol_land, sol_key)


def solution(mesh):
    split = Mesh(mesh.devices.reshape(4, 4, 4, 2), ("lm_0", "lm_1", "kf_0", "kf_1"))
    in_specs = (
        P(None, LM_KF),
        P(None, LM_KF),
        P(None, LM_KF),
        P(None, LM_KF),
        P(None, LM_KF),
        P(None, LM_KF),
        P(LM_KF),
        P(LM_KF),
        P(LM_KF),
        P(None, LM_KF),
    )
    out_specs = (P(None, LM_KF), P(None, LM_KF))
    return jax.shard_map(
        shards, mesh=split, in_specs=in_specs, out_specs=out_specs, check_vma=False
    )
```

```python
import functools

import jax
import jax.numpy as jnp
from jax import lax
from jax.experimental import pallas as pl
from jax.experimental.pallas import tpu as pltpu
from jax.sharding import Mesh
from jax.sharding import PartitionSpec as P

WSTATES = 16
SDIM = 15
BLOCK = 128
ITERS = 2
WPAR = 240
LOW = 256
CHUNK = 4096
KF = ("kf_0", "kf_1")
LM = ("lm_0", "lm_1")
LM_KF = ("lm_0", "lm_1", "kf_0", "kf_1")


def window_product(preint, vectors):
    windows = preint.shape[1] // WPAR
    stacked = vectors.reshape(SDIM, windows, WSTATES).transpose(1, 2, 0).reshape(windows * WPAR)
    owner = jnp.arange(windows * WPAR, dtype=jnp.int32) // WPAR
    spread = jnp.where(
        owner[:, None] == jnp.arange(windows, dtype=jnp.int32)[None, :], stacked[:, None], 0.0
    )
    mapped = jnp.dot(preint, spread, precision=lax.Precision.HIGH)
    return (
        mapped.reshape(WSTATES, SDIM, windows).transpose(1, 2, 0).reshape(SDIM, windows * WSTATES)
    )


def split_parts(value):
    high = value.astype(jnp.bfloat16)
    low = (value - high.astype(jnp.float32)).astype(jnp.bfloat16)
    return high, low


def table_parts(full):
    channels, extent = full.shape
    folded = full.reshape(channels * (extent // LOW), LOW)
    high = lax.reduce_precision(folded, exponent_bits=8, mantissa_bits=7)
    return jnp.concatenate(
        [high.astype(jnp.bfloat16), (folded - high).astype(jnp.bfloat16)], axis=1
    )


def in_order(blocks, dim):
    shape = list(blocks.shape[1:])
    shape[dim] *= blocks.shape[0]
    return jnp.moveaxis(blocks, 0, dim).reshape(shape)


def from_everyone(value, axis):
    copies = jnp.broadcast_to(value, (lax.axis_size(axis), *value.shape))
    return lax.all_to_all(copies, axis, split_axis=0, concat_axis=0, tiled=True)


def gather_directly(value, axis, dim):
    return in_order(from_everyone(value, axis), dim)


def split_up(value, dim, devices):
    before, after = (value.shape[:dim], value.shape[dim + 1 :])
    return jnp.moveaxis(value.reshape(*before, devices, -1, *after), dim, 0)


def sum_at_owner(value, axis, dim):
    blocks = split_up(value, dim, lax.axis_size(axis))
    arrived = lax.all_to_all(blocks, axis, split_axis=0, concat_axis=0, tiled=True)
    return arrived.sum(axis=0)


def sum_at_owner_with(value, scalars, axis):
    devices = lax.axis_size(axis)
    blocks = split_up(value, 1, devices)
    extra = jnp.zeros((devices, 1, blocks.shape[2]), jnp.float32)
    extra = extra.at[:, 0, : scalars.shape[0]].set(scalars[None, :])
    blocks = jnp.concatenate([blocks, extra], axis=1)
    arrived = lax.all_to_all(blocks, axis, split_axis=0, concat_axis=0, tiled=True).sum(axis=0)
    return arrived[:-1], arrived[-1, : scalars.shape[0]]


def make_observe_kernel(with_scatter):
    def kernel(valid_ref, lpos_ref, kpos_ref, ljac_ref, kjac_ref, ltab_ref, ktab_ref, *outs):
        if with_scatter:
            sq_ref, lacc_ref, kacc_ref = outs
        else:
            (sq_ref,) = outs
        step = pl.program_id(0)

        @pl.when(step == 0)
        def _():
            for ref in outs:
                ref[...] = jnp.zeros_like(ref)

        span = valid_ref.shape[1]
        land_high = ltab_ref.shape[0] // 3
        key_high = ktab_ref.shape[0] // SDIM
        lpos = lpos_ref[...]
        kpos = kpos_ref[...]
        land_hot = (
            lax.broadcasted_iota(jnp.int32, (LOW, span), 0) == lpos % LOW
        ).astype(jnp.bfloat16)
        key_hot = (
            lax.broadcasted_iota(jnp.int32, (LOW, span), 0) == kpos % LOW
        ).astype(jnp.bfloat16)
        land_sel = (
            lax.broadcasted_iota(jnp.int32, (land_high, span), 0) == lpos // LOW
        ).astype(jnp.float32)
        key_sel = (
            lax.broadcasted_iota(jnp.int32, (key_high, span), 0) == kpos // LOW
        ).astype(jnp.float32)

        def gather(tab_ref, hot, sel, channels, high):
            rows = jnp.dot(
                tab_ref[...], jnp.concatenate([hot, hot], axis=0),
                preferred_element_type=jnp.float32,
            )
            return [
                jnp.sum(rows[c * high:(c + 1) * high, :] * sel, axis=0, keepdims=True)
                for c in range(channels)
            ]

        seen_land = gather(ltab_ref, land_hot, land_sel, 3, land_high)
        seen_key = gather(ktab_ref, key_hot, key_sel, SDIM, key_high)
        ljac = ljac_ref[...]
        kjac = kjac_ref[...]
        valid = valid_ref[...]
        image = []
        for r in range(2):
            total = ljac[r * 3:r * 3 + 1, :] * seen_land[0]
            for c in range(1, 3):
                total = total + ljac[r * 3 + c:r * 3 + c + 1, :] * seen_land[c]
            for c in range(SDIM):
                total = total + kjac[r * SDIM + c:r * SDIM + c + 1, :] * seen_key[c]
            image.append(total * valid)
        sq_ref[...] += image[0] * image[0] + image[1] * image[1]
        if not with_scatter:
            return

        def scatter(acc_ref, jac, channels, hot, sel):
            mask = sel.astype(jnp.bfloat16)
            high_rows, low_rows = [], []
            for c in range(channels):
                back = jac[c:c + 1, :] * image[0] + jac[channels + c:channels + c + 1, :] * image[1]
                back_high, back_low = split_parts(back)
                high_rows.append(back_high * mask)
                low_rows.append(back_low * mask)
            high = jnp.concatenate(high_rows, axis=0)
            low = jnp.concatenate(low_rows, axis=0)
            dims = (((1,), (1,)), ((), ()))
            acc_ref[...] += lax.dot_general(
                high, hot, dims, preferred_element_type=jnp.float32
            ) + lax.dot_general(low, hot, dims, preferred_element_type=jnp.float32)

        scatter(lacc_ref, ljac, 3, land_hot, land_sel)
        scatter(kacc_ref, kjac, SDIM, key_hot, key_sel)

    return kernel


def observe(valid, land_pos, key_pos, land_jac, key_jac, land_full, key_full, with_scatter):
    count = land_jac.shape[1]
    ltab = table_parts(land_full)
    ktab = table_parts(key_full)
    row = lambda i: (0, i)
    whole = lambda i: (0, 0)
    out_specs = [pl.BlockSpec((1, CHUNK), whole)]
    out_shape = [jax.ShapeDtypeStruct((1, CHUNK), jnp.float32)]
    if with_scatter:
        out_specs += [
            pl.BlockSpec((ltab.shape[0], LOW), whole),
            pl.BlockSpec((ktab.shape[0], LOW), whole),
        ]
        out_shape += [
            jax.ShapeDtypeStruct((ltab.shape[0], LOW), jnp.float32),
            jax.ShapeDtypeStruct((ktab.shape[0], LOW), jnp.float32),
        ]
    outs = pl.pallas_call(
        make_observe_kernel(with_scatter),
        grid=(count // CHUNK,),
        in_specs=[
            pl.BlockSpec((1, CHUNK), row),
            pl.BlockSpec((1, CHUNK), row),
            pl.BlockSpec((1, CHUNK), row),
            pl.BlockSpec((land_jac.shape[0], CHUNK), row),
            pl.BlockSpec((key_jac.shape[0], CHUNK), row),
            pl.BlockSpec(ltab.shape, whole),
            pl.BlockSpec(ktab.shape, whole),
        ],
        out_specs=out_specs,
        out_shape=out_shape,
        compiler_params=pltpu.CompilerParams(dimension_semantics=("arbitrary",)),
    )(valid, land_pos, key_pos, land_jac, key_jac, ltab, ktab)
    if not with_scatter:
        return jnp.sum(outs[0]), None, None
    sq, lacc, kacc = outs
    return jnp.sum(sq), lacc.reshape(land_full.shape), kacc.reshape(key_full.shape)


def shards(
    land_rhs,
    key_rhs,
    land_damp,
    key_damp,
    land_jac,
    key_jac,
    obs_landmark,
    obs_keyframe,
    live_blocks,
    preint,
):
    state_dev = key_rhs.shape[1]
    kf_count = lax.axis_size(KF)
    count = obs_landmark.shape[0]
    owner_block = obs_keyframe // state_dev
    key_pos = (owner_block // kf_count * state_dev + obs_keyframe % state_dev).reshape(1, count)
    land_pos = obs_landmark.reshape(1, count)
    live = live_blocks[0]
    valid = (jnp.arange(count, dtype=jnp.int32) // BLOCK < live).astype(jnp.float32).reshape(1, count)

    def reduce_all(values):
        return from_everyone(jnp.stack(values), LM_KF).sum(axis=0)

    def image_norms(dir_land, dir_key, with_scatter):
        land_full = gather_directly(dir_land, KF, 1)
        key_full = gather_directly(dir_key, LM, 1)
        squared, summed_land, summed_key = observe(
            valid, land_pos, key_pos, land_jac, key_jac, land_full, key_full, with_scatter
        )
        windowed = window_product(preint, dir_key)
        local_rr = jnp.sum(dir_land * dir_land) + jnp.sum(dir_key * dir_key)
        local_product = (
            squared
            + jnp.sum(land_damp * dir_land * dir_land)
            + jnp.sum(dir_key * (key_damp * dir_key + windowed))
        )
        if not with_scatter:
            rr, product = reduce_all([local_rr, local_product])
            return rr, product, None, None
        owned_land, partial = sum_at_owner_with(
            summed_land, jnp.stack([local_rr, local_product]), KF
        )
        owned_key, total = sum_at_owner_with(summed_key, partial, LM)
        prod_land = owned_land + land_damp * dir_land
        prod_key = owned_key + key_damp * dir_key + windowed
        return total[0], total[1], prod_land, prod_key

    res_land, res_key = land_rhs, key_rhs
    norm_now, product, along_land, along_key = image_norms(res_land, res_key, True)
    step_size = norm_now / product
    sol_land = step_size * res_land
    sol_key = step_size * res_key
    dir_land, dir_key = res_land, res_key
    res_land = res_land - step_size * along_land
    res_key = res_key - step_size * along_key
    norm_next, product, _, _ = image_norms(res_land, res_key, False)
    beta_ratio = norm_next / norm_now
    step_size = norm_next / (product - beta_ratio * norm_next / step_size)
    dir_land = res_land + beta_ratio * dir_land
    dir_key = res_key + beta_ratio * dir_key
    sol_land = sol_land + step_size * dir_land
    sol_key = sol_key + step_size * dir_key
    return (sol_land, sol_key)


def solution(mesh):
    split = Mesh(mesh.devices.reshape(4, 4, 4, 2), ("lm_0", "lm_1", "kf_0", "kf_1"))
    in_specs = (
        P(None, LM_KF),
        P(None, LM_KF),
        P(None, LM_KF),
        P(None, LM_KF),
        P(None, LM_KF),
        P(None, LM_KF),
        P(LM_KF),
        P(LM_KF),
        P(LM_KF),
        P(None, LM_KF),
    )
    out_specs = (P(None, LM_KF), P(None, LM_KF))
    return jax.shard_map(
        shards, mesh=split, in_specs=in_specs, out_specs=out_specs, check_vma=False
    )
```

```python
import functools

import jax
import jax.numpy as jnp
from jax import lax
from jax.experimental import pallas as pl
from jax.experimental.pallas import tpu as pltpu
from jax.sharding import Mesh
from jax.sharding import PartitionSpec as P

WSTATES = 16
SDIM = 15
BLOCK = 128
ITERS = 2
WPAR = 240
LOW = 256
CHUNK = 4096
KF = ("kf_0", "kf_1")
LM = ("lm_0", "lm_1")
LM_KF = ("lm_0", "lm_1", "kf_0", "kf_1")


def window_product(preint, vectors):
    windows = preint.shape[1] // WPAR
    stacked = vectors.reshape(SDIM, windows, WSTATES).transpose(1, 2, 0).reshape(windows * WPAR)
    owner = jnp.arange(windows * WPAR, dtype=jnp.int32) // WPAR
    spread = jnp.where(
        owner[:, None] == jnp.arange(windows, dtype=jnp.int32)[None, :], stacked[:, None], 0.0
    )
    mapped = jnp.dot(preint, spread, precision=lax.Precision.HIGH)
    return (
        mapped.reshape(WSTATES, SDIM, windows).transpose(1, 2, 0).reshape(SDIM, windows * WSTATES)
    )


def split_parts(value):
    high = value.astype(jnp.bfloat16)
    low = (value - high.astype(jnp.float32)).astype(jnp.bfloat16)
    return high, low


def table_parts(full):
    channels, extent = full.shape
    folded = full.reshape(channels * (extent // LOW), LOW)
    high = lax.reduce_precision(folded, exponent_bits=8, mantissa_bits=7)
    return jnp.concatenate(
        [high.astype(jnp.bfloat16), (folded - high).astype(jnp.bfloat16)], axis=1
    )


def in_order(blocks, dim):
    shape = list(blocks.shape[1:])
    shape[dim] *= blocks.shape[0]
    return jnp.moveaxis(blocks, 0, dim).reshape(shape)


def from_everyone(value, axis):
    copies = jnp.broadcast_to(value, (lax.axis_size(axis), *value.shape))
    return lax.all_to_all(copies, axis, split_axis=0, concat_axis=0, tiled=True)


def gather_directly(value, axis, dim):
    return in_order(from_everyone(value, axis), dim)


def split_up(value, dim, devices):
    before, after = (value.shape[:dim], value.shape[dim + 1 :])
    return jnp.moveaxis(value.reshape(*before, devices, -1, *after), dim, 0)


def sum_at_owner(value, axis, dim):
    blocks = split_up(value, dim, lax.axis_size(axis))
    arrived = lax.all_to_all(blocks, axis, split_axis=0, concat_axis=0, tiled=True)
    return arrived.sum(axis=0)


def sum_at_owner_with(value, scalars, axis):
    devices = lax.axis_size(axis)
    blocks = split_up(value, 1, devices)
    extra = jnp.zeros((devices, 1, blocks.shape[2]), jnp.float32)
    extra = extra.at[:, 0, : scalars.shape[0]].set(scalars[None, :])
    blocks = jnp.concatenate([blocks, extra], axis=1)
    arrived = lax.all_to_all(blocks, axis, split_axis=0, concat_axis=0, tiled=True).sum(axis=0)
    return arrived[:-1], arrived[-1, : scalars.shape[0]]


def land_gather_kernel(lpos_ref, ltab_ref, seen_ref):
    span = lpos_ref.shape[1]
    land_high = ltab_ref.shape[0] // 3
    lpos = lpos_ref[...]
    land_hot = (
        lax.broadcasted_iota(jnp.int32, (LOW, span), 0) == lpos % LOW
    ).astype(jnp.bfloat16)
    land_sel = (
        lax.broadcasted_iota(jnp.int32, (land_high, span), 0) == lpos // LOW
    ).astype(jnp.float32)
    rows = jnp.dot(
        ltab_ref[...], jnp.concatenate([land_hot, land_hot], axis=0),
        preferred_element_type=jnp.float32,
    )
    seen_ref[...] = jnp.concatenate(
        [
            jnp.sum(rows[c * land_high:(c + 1) * land_high, :] * land_sel, axis=0, keepdims=True)
            for c in range(3)
        ],
        axis=0,
    )


def make_observe_kernel(with_scatter):
    def kernel(valid_ref, lpos_ref, kpos_ref, ljac_ref, kjac_ref, seen_ref, ltab_ref, ktab_ref, *outs):
        if with_scatter:
            sq_ref, lacc_ref, kacc_ref = outs
        else:
            (sq_ref,) = outs
        step = pl.program_id(0)

        @pl.when(step == 0)
        def _():
            for ref in outs:
                ref[...] = jnp.zeros_like(ref)

        span = valid_ref.shape[1]
        land_high = ltab_ref.shape[0] // 3
        key_high = ktab_ref.shape[0] // SDIM
        lpos = lpos_ref[...]
        kpos = kpos_ref[...]
        land_hot = (
            lax.broadcasted_iota(jnp.int32, (LOW, span), 0) == lpos % LOW
        ).astype(jnp.bfloat16)
        key_hot = (
            lax.broadcasted_iota(jnp.int32, (LOW, span), 0) == kpos % LOW
        ).astype(jnp.bfloat16)
        land_sel = (
            lax.broadcasted_iota(jnp.int32, (land_high, span), 0) == lpos // LOW
        ).astype(jnp.float32)
        key_sel = (
            lax.broadcasted_iota(jnp.int32, (key_high, span), 0) == kpos // LOW
        ).astype(jnp.float32)

        def gather(tab_ref, hot, sel, channels, high):
            rows = jnp.dot(
                tab_ref[...], jnp.concatenate([hot, hot], axis=0),
                preferred_element_type=jnp.float32,
            )
            return [
                jnp.sum(rows[c * high:(c + 1) * high, :] * sel, axis=0, keepdims=True)
                for c in range(channels)
            ]

        seen_all = seen_ref[...]
        seen_land = [seen_all[c:c + 1, :] for c in range(3)]
        seen_key = gather(ktab_ref, key_hot, key_sel, SDIM, key_high)
        ljac = ljac_ref[...]
        kjac = kjac_ref[...]
        valid = valid_ref[...]
        image = []
        for r in range(2):
            total = ljac[r * 3:r * 3 + 1, :] * seen_land[0]
            for c in range(1, 3):
                total = total + ljac[r * 3 + c:r * 3 + c + 1, :] * seen_land[c]
            for c in range(SDIM):
                total = total + kjac[r * SDIM + c:r * SDIM + c + 1, :] * seen_key[c]
            image.append(total * valid)
        sq_ref[...] += image[0] * image[0] + image[1] * image[1]
        if not with_scatter:
            return

        def scatter(acc_ref, jac, channels, hot, sel):
            mask = sel.astype(jnp.bfloat16)
            high_rows, low_rows = [], []
            for c in range(channels):
                back = jac[c:c + 1, :] * image[0] + jac[channels + c:channels + c + 1, :] * image[1]
                back_high, back_low = split_parts(back)
                high_rows.append(back_high * mask)
                low_rows.append(back_low * mask)
            high = jnp.concatenate(high_rows, axis=0)
            low = jnp.concatenate(low_rows, axis=0)
            dims = (((1,), (1,)), ((), ()))
            acc_ref[...] += lax.dot_general(
                high, hot, dims, preferred_element_type=jnp.float32
            ) + lax.dot_general(low, hot, dims, preferred_element_type=jnp.float32)

        scatter(lacc_ref, ljac, 3, land_hot, land_sel)
        scatter(kacc_ref, kjac, SDIM, key_hot, key_sel)

    return kernel


def observe(valid, land_pos, key_pos, land_jac, key_jac, land_full, key_full, with_scatter):
    count = land_jac.shape[1]
    ltab = table_parts(land_full)
    ktab = table_parts(key_full)
    row = lambda i: (0, i)
    whole = lambda i: (0, 0)
    out_specs = [pl.BlockSpec((1, CHUNK), whole)]
    out_shape = [jax.ShapeDtypeStruct((1, CHUNK), jnp.float32)]
    if with_scatter:
        out_specs += [
            pl.BlockSpec((ltab.shape[0], LOW), whole),
            pl.BlockSpec((ktab.shape[0], LOW), whole),
        ]
        out_shape += [
            jax.ShapeDtypeStruct((ltab.shape[0], LOW), jnp.float32),
            jax.ShapeDtypeStruct((ktab.shape[0], LOW), jnp.float32),
        ]
    seen_land = pl.pallas_call(
        land_gather_kernel,
        grid=(count // CHUNK,),
        in_specs=[pl.BlockSpec((1, CHUNK), row), pl.BlockSpec(ltab.shape, whole)],
        out_specs=pl.BlockSpec((3, CHUNK), row),
        out_shape=jax.ShapeDtypeStruct((3, count), jnp.float32),
        compiler_params=pltpu.CompilerParams(dimension_semantics=("arbitrary",)),
    )(land_pos, ltab)
    outs = pl.pallas_call(
        make_observe_kernel(with_scatter),
        grid=(count // CHUNK,),
        in_specs=[
            pl.BlockSpec((1, CHUNK), row),
            pl.BlockSpec((1, CHUNK), row),
            pl.BlockSpec((1, CHUNK), row),
            pl.BlockSpec((land_jac.shape[0], CHUNK), row),
            pl.BlockSpec((key_jac.shape[0], CHUNK), row),
            pl.BlockSpec((3, CHUNK), row),
            pl.BlockSpec(ltab.shape, whole),
            pl.BlockSpec(ktab.shape, whole),
        ],
        out_specs=out_specs,
        out_shape=out_shape,
        compiler_params=pltpu.CompilerParams(dimension_semantics=("arbitrary",)),
    )(valid, land_pos, key_pos, land_jac, key_jac, seen_land, ltab, ktab)
    if not with_scatter:
        return jnp.sum(outs[0]), None, None
    sq, lacc, kacc = outs
    return jnp.sum(sq), lacc.reshape(land_full.shape), kacc.reshape(key_full.shape)


def shards(
    land_rhs,
    key_rhs,
    land_damp,
    key_damp,
    land_jac,
    key_jac,
    obs_landmark,
    obs_keyframe,
    live_blocks,
    preint,
):
    state_dev = key_rhs.shape[1]
    kf_count = lax.axis_size(KF)
    count = obs_landmark.shape[0]
    owner_block = obs_keyframe // state_dev
    key_pos = (owner_block // kf_count * state_dev + obs_keyframe % state_dev).reshape(1, count)
    land_pos = obs_landmark.reshape(1, count)
    live = live_blocks[0]
    valid = (jnp.arange(count, dtype=jnp.int32) // BLOCK < live).astype(jnp.float32).reshape(1, count)

    def reduce_all(values):
        return from_everyone(jnp.stack(values), LM_KF).sum(axis=0)

    def image_norms(dir_land, dir_key, with_scatter):
        land_full = gather_directly(dir_land, KF, 1)
        key_full = gather_directly(dir_key, LM, 1)
        squared, summed_land, summed_key = observe(
            valid, land_pos, key_pos, land_jac, key_jac, land_full, key_full, with_scatter
        )
        windowed = window_product(preint, dir_key)
        local_rr = jnp.sum(dir_land * dir_land) + jnp.sum(dir_key * dir_key)
        local_product = (
            squared
            + jnp.sum(land_damp * dir_land * dir_land)
            + jnp.sum(dir_key * (key_damp * dir_key + windowed))
        )
        if not with_scatter:
            rr, product = reduce_all([local_rr, local_product])
            return rr, product, None, None
        owned_land, partial = sum_at_owner_with(
            summed_land, jnp.stack([local_rr, local_product]), KF
        )
        owned_key, total = sum_at_owner_with(summed_key, partial, LM)
        prod_land = owned_land + land_damp * dir_land
        prod_key = owned_key + key_damp * dir_key + windowed
        return total[0], total[1], prod_land, prod_key

    res_land, res_key = land_rhs, key_rhs
    norm_now, product, along_land, along_key = image_norms(res_land, res_key, True)
    step_size = norm_now / product
    sol_land = step_size * res_land
    sol_key = step_size * res_key
    dir_land, dir_key = res_land, res_key
    res_land = res_land - step_size * along_land
    res_key = res_key - step_size * along_key
    norm_next, product, _, _ = image_norms(res_land, res_key, False)
    beta_ratio = norm_next / norm_now
    step_size = norm_next / (product - beta_ratio * norm_next / step_size)
    dir_land = res_land + beta_ratio * dir_land
    dir_key = res_key + beta_ratio * dir_key
    sol_land = sol_land + step_size * dir_land
    sol_key = sol_key + step_size * dir_key
    return (sol_land, sol_key)


def solution(mesh):
    split = Mesh(mesh.devices.reshape(4, 4, 4, 2), ("lm_0", "lm_1", "kf_0", "kf_1"))
    in_specs = (
        P(None, LM_KF),
        P(None, LM_KF),
        P(None, LM_KF),
        P(None, LM_KF),
        P(None, LM_KF),
        P(None, LM_KF),
        P(LM_KF),
        P(LM_KF),
        P(LM_KF),
        P(None, LM_KF),
    )
    out_specs = (P(None, LM_KF), P(None, LM_KF))
    return jax.shard_map(
        shards, mesh=split, in_specs=in_specs, out_specs=out_specs, check_vma=False
    )
```

```python
import functools

import jax
import jax.numpy as jnp
from jax import lax
from jax.experimental import pallas as pl
from jax.experimental.pallas import tpu as pltpu
from jax.sharding import Mesh
from jax.sharding import PartitionSpec as P

WSTATES = 16
SDIM = 15
BLOCK = 128
ITERS = 2
WPAR = 240
LOW = 256
CHUNK = 4096
KF = ("kf_0", "kf_1")
LM = ("lm_0", "lm_1")
LM_KF = ("lm_0", "lm_1", "kf_0", "kf_1")


def window_product(preint, vectors):
    windows = preint.shape[1] // WPAR
    stacked = vectors.reshape(SDIM, windows, WSTATES).transpose(1, 2, 0).reshape(windows * WPAR)
    owner = jnp.arange(windows * WPAR, dtype=jnp.int32) // WPAR
    spread = jnp.where(
        owner[:, None] == jnp.arange(windows, dtype=jnp.int32)[None, :], stacked[:, None], 0.0
    )
    mapped = jnp.dot(preint, spread, precision=lax.Precision.HIGH)
    return (
        mapped.reshape(WSTATES, SDIM, windows).transpose(1, 2, 0).reshape(SDIM, windows * WSTATES)
    )


def split_parts(value):
    high = value.astype(jnp.bfloat16)
    low = (value - high.astype(jnp.float32)).astype(jnp.bfloat16)
    return high, low


def table_parts(full):
    channels, extent = full.shape
    folded = full.reshape(channels * (extent // LOW), LOW)
    high = lax.reduce_precision(folded, exponent_bits=8, mantissa_bits=7)
    return jnp.concatenate(
        [high.astype(jnp.bfloat16), (folded - high).astype(jnp.bfloat16)], axis=1
    )


def in_order(blocks, dim):
    shape = list(blocks.shape[1:])
    shape[dim] *= blocks.shape[0]
    return jnp.moveaxis(blocks, 0, dim).reshape(shape)


def from_everyone(value, axis):
    copies = jnp.broadcast_to(value, (lax.axis_size(axis), *value.shape))
    return lax.all_to_all(copies, axis, split_axis=0, concat_axis=0, tiled=True)


def gather_directly(value, axis, dim):
    return in_order(from_everyone(value, axis), dim)


def split_up(value, dim, devices):
    before, after = (value.shape[:dim], value.shape[dim + 1 :])
    return jnp.moveaxis(value.reshape(*before, devices, -1, *after), dim, 0)


def sum_at_owner(value, axis, dim):
    blocks = split_up(value, dim, lax.axis_size(axis))
    arrived = lax.all_to_all(blocks, axis, split_axis=0, concat_axis=0, tiled=True)
    return arrived.sum(axis=0)


def sum_at_owner_with(value, scalars, axis):
    devices = lax.axis_size(axis)
    blocks = split_up(value, 1, devices)
    extra = jnp.zeros((devices, 1, blocks.shape[2]), jnp.float32)
    extra = extra.at[:, 0, : scalars.shape[0]].set(scalars[None, :])
    blocks = jnp.concatenate([blocks, extra], axis=1)
    arrived = lax.all_to_all(blocks, axis, split_axis=0, concat_axis=0, tiled=True).sum(axis=0)
    return arrived[:-1], arrived[-1, : scalars.shape[0]]


def land_gather_kernel(lpos_ref, ltab_ref, seen_ref):
    span = lpos_ref.shape[1]
    land_high = ltab_ref.shape[0] // 3
    lpos = lpos_ref[...]
    land_hot = (
        lax.broadcasted_iota(jnp.int32, (LOW, span), 0) == lpos % LOW
    ).astype(jnp.bfloat16)
    land_sel = (
        lax.broadcasted_iota(jnp.int32, (land_high, span), 0) == lpos // LOW
    ).astype(jnp.float32)
    rows = jnp.dot(
        ltab_ref[...], jnp.concatenate([land_hot, land_hot], axis=0),
        preferred_element_type=jnp.float32,
    )
    seen_ref[...] = jnp.concatenate(
        [
            jnp.sum(rows[c * land_high:(c + 1) * land_high, :] * land_sel, axis=0, keepdims=True)
            for c in range(3)
        ],
        axis=0,
    )


def scatter_into(acc_ref, jac, channels, hot, sel, image):
    mask = sel.astype(jnp.bfloat16)
    high_rows, low_rows = [], []
    for c in range(channels):
        back = jac[c:c + 1, :] * image[0] + jac[channels + c:channels + c + 1, :] * image[1]
        back_high, back_low = split_parts(back)
        high_rows.append(back_high * mask)
        low_rows.append(back_low * mask)
    high = jnp.concatenate(high_rows, axis=0)
    low = jnp.concatenate(low_rows, axis=0)
    dims = (((1,), (1,)), ((), ()))
    acc_ref[...] += lax.dot_general(
        high, hot, dims, preferred_element_type=jnp.float32
    ) + lax.dot_general(low, hot, dims, preferred_element_type=jnp.float32)


def key_scatter_kernel(kpos_ref, kjac_ref, image_ref, ktab_ref, kacc_ref):
    @pl.when(pl.program_id(0) == 0)
    def _():
        kacc_ref[...] = jnp.zeros_like(kacc_ref)

    span = kpos_ref.shape[1]
    key_high = ktab_ref.shape[0] // SDIM
    kpos = kpos_ref[...]
    key_hot = (
        lax.broadcasted_iota(jnp.int32, (LOW, span), 0) == kpos % LOW
    ).astype(jnp.bfloat16)
    key_sel = (
        lax.broadcasted_iota(jnp.int32, (key_high, span), 0) == kpos // LOW
    ).astype(jnp.float32)
    image_all = image_ref[...]
    scatter_into(kacc_ref, kjac_ref[...], SDIM, key_hot, key_sel, [image_all[0:1, :], image_all[1:2, :]])


def make_observe_kernel(with_scatter):
    def kernel(valid_ref, lpos_ref, kpos_ref, ljac_ref, kjac_ref, seen_ref, ltab_ref, ktab_ref, *outs):
        if with_scatter:
            sq_ref, image_ref, lacc_ref = outs
        else:
            (sq_ref,) = outs
        step = pl.program_id(0)

        @pl.when(step == 0)
        def _():
            sq_ref[...] = jnp.zeros_like(sq_ref)
            if with_scatter:
                lacc_ref[...] = jnp.zeros_like(lacc_ref)

        span = valid_ref.shape[1]
        land_high = ltab_ref.shape[0] // 3
        key_high = ktab_ref.shape[0] // SDIM
        lpos = lpos_ref[...]
        kpos = kpos_ref[...]
        land_hot = (
            lax.broadcasted_iota(jnp.int32, (LOW, span), 0) == lpos % LOW
        ).astype(jnp.bfloat16)
        key_hot = (
            lax.broadcasted_iota(jnp.int32, (LOW, span), 0) == kpos % LOW
        ).astype(jnp.bfloat16)
        land_sel = (
            lax.broadcasted_iota(jnp.int32, (land_high, span), 0) == lpos // LOW
        ).astype(jnp.float32)
        key_sel = (
            lax.broadcasted_iota(jnp.int32, (key_high, span), 0) == kpos // LOW
        ).astype(jnp.float32)

        def gather(tab_ref, hot, sel, channels, high):
            rows = jnp.dot(
                tab_ref[...], jnp.concatenate([hot, hot], axis=0),
                preferred_element_type=jnp.float32,
            )
            return [
                jnp.sum(rows[c * high:(c + 1) * high, :] * sel, axis=0, keepdims=True)
                for c in range(channels)
            ]

        seen_all = seen_ref[...]
        seen_land = [seen_all[c:c + 1, :] for c in range(3)]
        seen_key = gather(ktab_ref, key_hot, key_sel, SDIM, key_high)
        ljac = ljac_ref[...]
        kjac = kjac_ref[...]
        valid = valid_ref[...]
        image = []
        for r in range(2):
            total = ljac[r * 3:r * 3 + 1, :] * seen_land[0]
            for c in range(1, 3):
                total = total + ljac[r * 3 + c:r * 3 + c + 1, :] * seen_land[c]
            for c in range(SDIM):
                total = total + kjac[r * SDIM + c:r * SDIM + c + 1, :] * seen_key[c]
            image.append(total * valid)
        sq_ref[...] += image[0] * image[0] + image[1] * image[1]
        if not with_scatter:
            return

        image_ref[...] = jnp.concatenate(image, axis=0)
        scatter_into(lacc_ref, ljac, 3, land_hot, land_sel, image)

    return kernel


def observe(valid, land_pos, key_pos, land_jac, key_jac, land_full, key_full, with_scatter):
    count = land_jac.shape[1]
    ltab = table_parts(land_full)
    ktab = table_parts(key_full)
    row = lambda i: (0, i)
    whole = lambda i: (0, 0)
    out_specs = [pl.BlockSpec((1, CHUNK), whole)]
    out_shape = [jax.ShapeDtypeStruct((1, CHUNK), jnp.float32)]
    if with_scatter:
        out_specs += [
            pl.BlockSpec((2, CHUNK), row),
            pl.BlockSpec((ltab.shape[0], LOW), whole),
        ]
        out_shape += [
            jax.ShapeDtypeStruct((2, count), jnp.float32),
            jax.ShapeDtypeStruct((ltab.shape[0], LOW), jnp.float32),
        ]
    seen_land = pl.pallas_call(
        land_gather_kernel,
        grid=(count // CHUNK,),
        in_specs=[pl.BlockSpec((1, CHUNK), row), pl.BlockSpec(ltab.shape, whole)],
        out_specs=pl.BlockSpec((3, CHUNK), row),
        out_shape=jax.ShapeDtypeStruct((3, count), jnp.float32),
        compiler_params=pltpu.CompilerParams(dimension_semantics=("arbitrary",)),
    )(land_pos, ltab)
    outs = pl.pallas_call(
        make_observe_kernel(with_scatter),
        grid=(count // CHUNK,),
        in_specs=[
            pl.BlockSpec((1, CHUNK), row),
            pl.BlockSpec((1, CHUNK), row),
            pl.BlockSpec((1, CHUNK), row),
            pl.BlockSpec((land_jac.shape[0], CHUNK), row),
            pl.BlockSpec((key_jac.shape[0], CHUNK), row),
            pl.BlockSpec((3, CHUNK), row),
            pl.BlockSpec(ltab.shape, whole),
            pl.BlockSpec(ktab.shape, whole),
        ],
        out_specs=out_specs,
        out_shape=out_shape,
        compiler_params=pltpu.CompilerParams(dimension_semantics=("arbitrary",)),
    )(valid, land_pos, key_pos, land_jac, key_jac, seen_land, ltab, ktab)
    if not with_scatter:
        return jnp.sum(outs[0]), None, None
    sq, image, lacc = outs
    kacc = pl.pallas_call(
        key_scatter_kernel,
        grid=(count // CHUNK,),
        in_specs=[
            pl.BlockSpec((1, CHUNK), row),
            pl.BlockSpec((key_jac.shape[0], CHUNK), row),
            pl.BlockSpec((2, CHUNK), row),
            pl.BlockSpec(ktab.shape, whole),
        ],
        out_specs=pl.BlockSpec((ktab.shape[0], LOW), whole),
        out_shape=jax.ShapeDtypeStruct((ktab.shape[0], LOW), jnp.float32),
        compiler_params=pltpu.CompilerParams(dimension_semantics=("arbitrary",)),
    )(key_pos, key_jac, image, ktab)
    return jnp.sum(sq), lacc.reshape(land_full.shape), kacc.reshape(key_full.shape)


def shards(
    land_rhs,
    key_rhs,
    land_damp,
    key_damp,
    land_jac,
    key_jac,
    obs_landmark,
    obs_keyframe,
    live_blocks,
    preint,
):
    state_dev = key_rhs.shape[1]
    kf_count = lax.axis_size(KF)
    count = obs_landmark.shape[0]
    owner_block = obs_keyframe // state_dev
    key_pos = (owner_block // kf_count * state_dev + obs_keyframe % state_dev).reshape(1, count)
    land_pos = obs_landmark.reshape(1, count)
    live = live_blocks[0]
    valid = (jnp.arange(count, dtype=jnp.int32) // BLOCK < live).astype(jnp.float32).reshape(1, count)

    def reduce_all(values):
        return from_everyone(jnp.stack(values), LM_KF).sum(axis=0)

    def image_norms(dir_land, dir_key, with_scatter):
        land_full = gather_directly(dir_land, KF, 1)
        key_full = gather_directly(dir_key, LM, 1)
        squared, summed_land, summed_key = observe(
            valid, land_pos, key_pos, land_jac, key_jac, land_full, key_full, with_scatter
        )
        windowed = window_product(preint, dir_key)
        local_rr = jnp.sum(dir_land * dir_land) + jnp.sum(dir_key * dir_key)
        local_product = (
            squared
            + jnp.sum(land_damp * dir_land * dir_land)
            + jnp.sum(dir_key * (key_damp * dir_key + windowed))
        )
        if not with_scatter:
            rr, product = reduce_all([local_rr, local_product])
            return rr, product, None, None
        owned_land, partial = sum_at_owner_with(
            summed_land, jnp.stack([local_rr, local_product]), KF
        )
        owned_key, total = sum_at_owner_with(summed_key, partial, LM)
        prod_land = owned_land + land_damp * dir_land
        prod_key = owned_key + key_damp * dir_key + windowed
        return total[0], total[1], prod_land, prod_key

    res_land, res_key = land_rhs, key_rhs
    norm_now, product, along_land, along_key = image_norms(res_land, res_key, True)
    step_size = norm_now / product
    sol_land = step_size * res_land
    sol_key = step_size * res_key
    dir_land, dir_key = res_land, res_key
    res_land = res_land - step_size * along_land
    res_key = res_key - step_size * along_key
    norm_next, product, _, _ = image_norms(res_land, res_key, False)
    beta_ratio = norm_next / norm_now
    step_size = norm_next / (product - beta_ratio * norm_next / step_size)
    dir_land = res_land + beta_ratio * dir_land
    dir_key = res_key + beta_ratio * dir_key
    sol_land = sol_land + step_size * dir_land
    sol_key = sol_key + step_size * dir_key
    return (sol_land, sol_key)


def solution(mesh):
    split = Mesh(mesh.devices.reshape(4, 4, 4, 2), ("lm_0", "lm_1", "kf_0", "kf_1"))
    in_specs = (
        P(None, LM_KF),
        P(None, LM_KF),
        P(None, LM_KF),
        P(None, LM_KF),
        P(None, LM_KF),
        P(None, LM_KF),
        P(LM_KF),
        P(LM_KF),
        P(LM_KF),
        P(None, LM_KF),
    )
    out_specs = (P(None, LM_KF), P(None, LM_KF))
    return jax.shard_map(
        shards, mesh=split, in_specs=in_specs, out_specs=out_specs, check_vma=False
    )
```
